128 devices in a mesh: req: 32 (over z, x, y_hi), tp: 4 (over y_lo, core).
Axes of the slice: x: 4, y: 4 (y_hi: 2, y_lo: 2; y = y_hi * 2 + y_lo), z: 4, core: 2. Of those that a mesh axis runs over, the one named last changes fastest.
Arguments:
- hidden_in: bfloat16 [64, 512, 1280], P('req'), may hold values from -6 to 6
- lengths: int32 [64], P('req'), may hold values from 128 to 512, as said below
- attn_gain: float32 [1280], replicated, may hold values from 0.1 to 1.9
- mlp_gain: float32 [1280], replicated, may hold values from 0.1 to 1.9
- q_master: float32 [1280, 1280], P(('req', 'tp')), may hold values from -1 to 1
- k_master: float32 [1280, 320], P(('req', 'tp')), may hold values from -1 to 1
- trainer_value_weight: float32 [1280, 320], P(('req', 'tp')), may hold values from -0.15625 to 0.15625
- o_master: float32 [1280, 1280], P(('req', 'tp')), may hold values from -0.15625 to 0.15625
- gate_master: float32 [1280, 3584], P(('req', 'tp')), may hold values from -0.15625 to 0.15625
- up_master: float32 [1280, 3584], P(('req', 'tp')), may hold values from -0.15625 to 0.15625
- down_master: float32 [3584, 1280], P(('req', 'tp')), may hold values from -0.09375 to 0.09375
Outputs:
- hidden_out: bfloat16 [64, 512, 1280], P('req')
- kv_cache: bfloat16 [64, 512, 640], P('req')
The draws below stay inside these ranges and needn't reach their ends.
Inputs may be any that keep to these rules, and one draw needn't show every extreme that they name: `lengths`: each prompt has at least a quarter of 512 real tokens; in every draw some prompt has exactly 512.
All inputs are finite; a program needn't handle non-finite values.
Results may differ from the reference program's by a relative error of at most 0.012.
Values may be sent and summed in bfloat16 or wider, within the bound.
No kernel may reach another device: no remote copies, remote signals or barrier semaphores. Data moves between devices by JAX's collectives and lax.ppermute only.
A program may use at most 192 MiB of HBM per device.

```python
import math
import jax
import jax.numpy as jnp
from jax import lax

MODEL_DIM = 1280
FF = 3584
QUERY_HEADS = 20
KEY_VALUE_HEADS = 5
HEAD_DIM = 64
PROMPT_LENGTH = 512
PROMPTS = 64
N_TP = 4


def draw_lengths(key, part):
    base_len = jax.random.randint(jax.random.fold_in(key, 11), (PROMPTS,), PROMPT_LENGTH // 4, PROMPT_LENGTH + 1)
    chosen = jax.random.randint(jax.random.fold_in(key, 12), (), 0, PROMPTS)
    return jnp.where(jnp.arange(PROMPTS) == chosen, PROMPT_LENGTH, base_len).astype(jnp.int32)


def unsharded_weight(key, salt, columns):
    raw = jax.random.normal(jax.random.fold_in(key, salt), (MODEL_DIM, columns), jnp.float32)
    return jnp.clip(raw, -6.0, 6.0) / math.sqrt(MODEL_DIM)


def draw_q_master(key, part):
    weight_table = unsharded_weight(key, 31, QUERY_HEADS * HEAD_DIM)
    return weight_table


def draw_k_master(key, part):
    weight_table = unsharded_weight(key, 32, KEY_VALUE_HEADS * HEAD_DIM)
    return weight_table


def draw_hidden_in(key, part):
    rows = jnp.clip(jax.random.normal(jax.random.fold_in(key, 33), (PROMPTS, PROMPT_LENGTH, MODEL_DIM), jnp.float32), -6.0, 6.0)
    return rows.astype(jnp.bfloat16)


def block_scale(rng, extent, shards, low, high):
    loudness, own = 1.0, jax.random.fold_in(rng, 6)
    for dim, blocks in shards:
        draws = jnp.exp(jax.random.uniform(jax.random.fold_in(own, dim), (blocks,), jnp.float32, low / len(shards), high / len(shards)))
        loudness = loudness * jnp.repeat(draws, extent[dim] // blocks).reshape([-1 if axis == dim else 1 for axis in range(len(extent))])
    return loudness


def gaussian(own_key, shape, scale, bound, split=(), kind=jnp.bfloat16):
    factor_of = block_scale(own_key, shape, split, -0.22, 0.18) if split else 1.0
    entries = jax.random.normal(own_key, shape, jnp.float32) * scale * factor_of
    return jnp.minimum(jnp.maximum(entries, -bound), bound).astype(kind)


def setup_inputs(seed: int = 0) -> dict:
    key_of = jax.random.split(jax.random.key(seed), 12)
    return {
        "hidden_in": draw_hidden_in(jax.random.fold_in(key_of[11], 71), 0),
        "lengths": draw_lengths(jax.random.fold_in(key_of[11], 71), 0),
        "attn_gain": jnp.clip(1.0 + 0.18 * jax.random.normal(key_of[2], (MODEL_DIM,), jnp.float32), 0.1, 1.9),
        "mlp_gain": jnp.clip(1.0 + 0.18 * jax.random.normal(key_of[3], (MODEL_DIM,), jnp.float32), 0.1, 1.9),
        "q_master": draw_q_master(jax.random.fold_in(key_of[11], 71), 0),
        "k_master": draw_k_master(jax.random.fold_in(key_of[11], 71), 0),
        "trainer_value_weight": gaussian(key_of[6], (MODEL_DIM, KEY_VALUE_HEADS * HEAD_DIM), MODEL_DIM ** -0.5, 0.15625, ((0, 128),), jnp.float32),
        "o_master": gaussian(key_of[7], (QUERY_HEADS * HEAD_DIM, MODEL_DIM), (QUERY_HEADS * HEAD_DIM) ** -0.5, 0.15625, ((0, 128),), jnp.float32),
        "gate_master": gaussian(key_of[8], (MODEL_DIM, FF), MODEL_DIM ** -0.5, 0.15625, ((0, 128),), jnp.float32),
        "up_master": gaussian(key_of[9], (MODEL_DIM, FF), MODEL_DIM ** -0.5, 0.15625, ((0, 128),), jnp.float32),
        "down_master": gaussian(key_of[10], (FF, MODEL_DIM), FF ** -0.5, 0.09375, ((0, 128),), jnp.float32),
    }


def rms_norm(field, gain_vec):
    scale = lax.rsqrt(lax.optimization_barrier(jnp.mean(field * field, axis=-1, keepdims=True)) + 1e-05)
    return (field * scale * gain_vec).astype(jnp.bfloat16)

def rope_tables(sequence_length, head_size):
    half_width = head_size // 2
    positions = jnp.arange(sequence_length, dtype=jnp.float32)[:, None]
    frequency = jnp.exp(-math.log(10000.0) * (2.0 * jnp.arange(half_width, dtype=jnp.float32) / head_size))
    angles = positions * frequency[None, :]
    return (jnp.cos(angles), jnp.sin(angles))

def rotate(field, cosine_table, sine_table):
    half_width = field.shape[-1] // 2
    first_half = field[..., :half_width]
    second_half = field[..., half_width:]
    cos_b = cosine_table[:, None, :]
    sin_b = sine_table[:, None, :]
    return jnp.concatenate([first_half * cos_b - second_half * sin_b, second_half * cos_b + first_half * sin_b], axis=-1)

def block_sum(left, weight_rows):
    row_count, inner = left.shape
    split_left = left.reshape(row_count, N_TP, inner // N_TP).astype(jnp.float32)
    split_right = weight_rows.reshape(N_TP, inner // N_TP, weight_rows.shape[1]).astype(jnp.float32)
    partial_value = jnp.einsum('snk,nkd->nsd', split_left, split_right)
    rounded = lax.optimization_barrier(partial_value.astype(jnp.bfloat16))
    return lax.optimization_barrier(jnp.sum(rounded.astype(jnp.float32), axis=0))

def reference(hidden_in, lengths, attn_gain, mlp_gain, q_master, k_master, trainer_value_weight, o_master, gate_master, up_master, down_master):
    q_w = q_master.astype(jnp.bfloat16)
    key_matrix = k_master.astype(jnp.bfloat16)
    value_matrix = trainer_value_weight.astype(jnp.bfloat16)
    o_w = o_master.astype(jnp.bfloat16)
    gate_w = gate_master.astype(jnp.bfloat16)
    up_w = up_master.astype(jnp.bfloat16)
    down_w = down_master.astype(jnp.bfloat16)
    cosine_table, sine_table = rope_tables(PROMPT_LENGTH, HEAD_DIM)
    group_width = QUERY_HEADS // KEY_VALUE_HEADS

    def one_prompt(prompt_item):
        field, length = prompt_item
        rows_f = field.astype(jnp.float32)
        normalized_input = rms_norm(rows_f, attn_gain)
        queries = jnp.dot(normalized_input, q_w, preferred_element_type=jnp.float32).reshape(PROMPT_LENGTH, QUERY_HEADS, HEAD_DIM)
        key_rows = jnp.dot(normalized_input, key_matrix, preferred_element_type=jnp.float32).reshape(PROMPT_LENGTH, KEY_VALUE_HEADS, HEAD_DIM)
        value_rows = jnp.dot(normalized_input, value_matrix, preferred_element_type=jnp.float32).reshape(PROMPT_LENGTH, KEY_VALUE_HEADS, HEAD_DIM)
        q_rot = rotate(queries, cosine_table, sine_table).astype(jnp.bfloat16)
        rotated_keys = rotate(key_rows, cosine_table, sine_table).astype(jnp.bfloat16)
        value_halves = value_rows.astype(jnp.bfloat16)
        cache_entries = jnp.concatenate([rotated_keys.reshape(PROMPT_LENGTH, KEY_VALUE_HEADS * HEAD_DIM), value_halves.reshape(PROMPT_LENGTH, KEY_VALUE_HEADS * HEAD_DIM)], axis=1)
        k_all = jnp.repeat(rotated_keys, group_width, axis=1).astype(jnp.float32)
        v_all = jnp.repeat(value_halves, group_width, axis=1).astype(jnp.float32)
        scores = jnp.einsum('qhd,khd->hqk', q_rot.astype(jnp.float32), k_all) / math.sqrt(HEAD_DIM)
        row_index = jnp.arange(PROMPT_LENGTH, dtype=jnp.int32)[:, None]
        col_index = jnp.arange(PROMPT_LENGTH, dtype=jnp.int32)[None, :]
        allowed = (col_index <= row_index) & (col_index < length)
        scores = jnp.where(allowed[None], scores, -1e+30)
        highest = lax.optimization_barrier(jnp.max(scores, axis=-1, keepdims=True))
        expo = jnp.exp(scores - highest)
        weight_table = (expo / lax.optimization_barrier(jnp.sum(expo, axis=-1, keepdims=True))).astype(jnp.bfloat16)
        attended = jnp.einsum('hqk,khd->qhd', weight_table.astype(jnp.float32), v_all).astype(jnp.bfloat16).reshape(PROMPT_LENGTH, QUERY_HEADS * HEAD_DIM)
        middle = rows_f + block_sum(attended, o_w)
        normed2 = rms_norm(middle, mlp_gain)
        gate_val = jnp.dot(normed2, gate_w, preferred_element_type=jnp.float32)
        up_val = jnp.dot(normed2, up_w, preferred_element_type=jnp.float32)
        hidden_ff = (jax.nn.silu(gate_val) * up_val).astype(jnp.bfloat16)
        result = (middle + block_sum(hidden_ff, down_w)).astype(jnp.bfloat16)
        return (result, cache_entries)
    hidden_out, kv_cache = lax.map(one_prompt, (hidden_in, lengths))
    return (hidden_out, kv_cache)
```

```python
import math

import jax
import jax.numpy as jnp
from jax import lax
from jax.sharding import PartitionSpec as P

QUERY_HEADS = 20
KEY_VALUE_HEADS = 5
HEAD_DIM = 64


def rms_norm(field, gain_vec):
    scale = lax.rsqrt(jnp.mean(field * field, axis=-1, keepdims=True) + 1e-05)
    return (field * scale * gain_vec).astype(jnp.bfloat16)


def rope_tables(sequence_length, head_size):
    half_width = head_size // 2
    positions = jnp.arange(sequence_length, dtype=jnp.float32)[:, None]
    frequency = jnp.exp(
        -math.log(10000.0) * (2.0 * jnp.arange(half_width, dtype=jnp.float32) / head_size)
    )
    angles = positions * frequency[None, :]
    return (jnp.cos(angles), jnp.sin(angles))


def rotate(field, cosine_table, sine_table):
    half_width = field.shape[-1] // 2
    first_half = field[..., :half_width]
    second_half = field[..., half_width:]
    cos_b = cosine_table[:, None, :]
    sin_b = sine_table[:, None, :]
    return jnp.concatenate(
        [first_half * cos_b - second_half * sin_b, second_half * cos_b + first_half * sin_b],
        axis=-1,
    )


def local(
    hidden_in,
    lengths,
    attn_gain,
    mlp_gain,
    q_master,
    k_master,
    trainer_value_weight,
    o_master,
    gate_master,
    up_master,
    down_master,
):
    tp_count = lax.axis_size("tp")
    req_count = lax.axis_size("req")
    tensor_shard_index = lax.axis_index("tp")
    bf = jnp.bfloat16
    q_cols = q_master.shape[1] // tp_count
    kv_cols = k_master.shape[1]
    ff_cols = gate_master.shape[1] // tp_count
    local_rows = q_master.shape[0]

    def dest_chunk(dest):
        return jnp.concatenate(
            [
                q_master[:, dest * q_cols : (dest + 1) * q_cols],
                k_master,
                trainer_value_weight,
                gate_master[:, dest * ff_cols : (dest + 1) * ff_cols],
                up_master[:, dest * ff_cols : (dest + 1) * ff_cols],
            ],
            axis=1,
        ).astype(bf)

    send = jnp.stack([dest_chunk(d) for d in range(tp_count)])
    recv = lax.all_to_all(send, "tp", 0, 0, tiled=False)
    col_block = recv.reshape(tp_count * local_rows, -1)

    row_pack = jnp.concatenate([o_master.reshape(-1), down_master.reshape(-1)]).astype(bf)
    per_block = req_count // tp_count
    perm = []
    for r_src in range(req_count):
        for t_src in range(tp_count):
            r_dst = tp_count * (r_src % per_block) + t_src
            t_dst = r_src // per_block
            perm.append((r_src * tp_count + t_src, r_dst * tp_count + t_dst))
    row_pack = lax.ppermute(row_pack, ("req", "tp"), perm)

    packed = jnp.concatenate([col_block.reshape(-1), row_pack])
    gathered = lax.all_gather(packed, "req", axis=0, tiled=False)
    col_size = col_block.size
    all_cols = gathered[:, :col_size].reshape(-1, col_block.shape[1])
    offs = [0, q_cols, q_cols + kv_cols, q_cols + 2 * kv_cols, q_cols + 2 * kv_cols + ff_cols]
    query_weight = all_cols[:, offs[0] : offs[1]]
    key_weight = all_cols[:, offs[1] : offs[2]]
    value_weight = all_cols[:, offs[2] : offs[3]]
    gate_weight = all_cols[:, offs[3] : offs[4]]
    up_weight = all_cols[:, offs[4] : offs[4] + ff_cols]
    o_size = o_master.size
    model_cols = o_master.shape[1]
    out_weight = gathered[:, col_size : col_size + o_size].reshape(-1, model_cols)
    down_weight = gathered[:, col_size + o_size :].reshape(-1, model_cols)
    prompt_batch, sequence_length, model_width = hidden_in.shape
    tok_rows = prompt_batch * sequence_length
    flat_rows = hidden_in.reshape(tok_rows, model_width).astype(jnp.float32)
    normalized_input = rms_norm(flat_rows, attn_gain)
    local_heads = query_weight.shape[1] // HEAD_DIM
    queries = jnp.dot(normalized_input, query_weight, preferred_element_type=jnp.float32).reshape(
        prompt_batch, sequence_length, local_heads, HEAD_DIM
    )
    key_rows = jnp.dot(normalized_input, key_weight, preferred_element_type=jnp.float32).reshape(
        prompt_batch, sequence_length, KEY_VALUE_HEADS, HEAD_DIM
    )
    value_rows = jnp.dot(
        normalized_input, value_weight, preferred_element_type=jnp.float32
    ).reshape(prompt_batch, sequence_length, KEY_VALUE_HEADS, HEAD_DIM)
    cosine_table, sine_table = rope_tables(sequence_length, HEAD_DIM)
    q_rot = rotate(queries, cosine_table, sine_table).astype(jnp.bfloat16)
    rotated_keys = rotate(key_rows, cosine_table, sine_table).astype(jnp.bfloat16)
    value_halves = value_rows.astype(jnp.bfloat16)
    kv_cache = jnp.concatenate(
        [
            rotated_keys.reshape(prompt_batch, sequence_length, KEY_VALUE_HEADS * HEAD_DIM),
            value_halves.reshape(prompt_batch, sequence_length, KEY_VALUE_HEADS * HEAD_DIM),
        ],
        axis=2,
    )
    owner_shards = (
        tensor_shard_index * local_heads + jnp.arange(local_heads, dtype=jnp.int32)
    ) // (QUERY_HEADS // KEY_VALUE_HEADS)
    selector_mask = (
        owner_shards[:, None] == jnp.arange(KEY_VALUE_HEADS, dtype=jnp.int32)[None, :]
    ).astype(jnp.bfloat16)
    k_local = jnp.einsum(
        "pshd,gh->psgd", rotated_keys, selector_mask, preferred_element_type=jnp.float32
    ).astype(jnp.bfloat16)
    v_local = jnp.einsum(
        "pshd,gh->psgd", value_halves, selector_mask, preferred_element_type=jnp.float32
    ).astype(jnp.bfloat16)
    scores = jnp.einsum(
        "pqhd,pkhd->phqk", q_rot, k_local, preferred_element_type=jnp.float32
    ) / math.sqrt(HEAD_DIM)
    row_index = jnp.arange(sequence_length, dtype=jnp.int32)[:, None]
    col_index = jnp.arange(sequence_length, dtype=jnp.int32)[None, :]
    allowed = (col_index <= row_index)[None, None] & (
        col_index[None, None] < lengths[:, None, None, None]
    )
    scores = jnp.where(allowed, scores, -1e30)
    highest = jnp.max(scores, axis=-1, keepdims=True)
    expo = jnp.exp(scores - highest)
    weight_table = (expo / jnp.sum(expo, axis=-1, keepdims=True)).astype(jnp.bfloat16)
    attended = (
        jnp.einsum("phqk,pkhd->pqhd", weight_table, v_local, preferred_element_type=jnp.float32)
        .astype(jnp.bfloat16)
        .reshape(tok_rows, local_heads * HEAD_DIM)
    )
    attn_total = lax.psum(
        jnp.dot(attended, out_weight, preferred_element_type=jnp.float32).astype(jnp.bfloat16), "tp"
    ).astype(jnp.float32)
    middle = flat_rows + attn_total
    normed_rows = rms_norm(middle, mlp_gain)
    gate_val = jnp.dot(normed_rows, gate_weight, preferred_element_type=jnp.float32)
    up_val = jnp.dot(normed_rows, up_weight, preferred_element_type=jnp.float32)
    hidden_ff = (jax.nn.silu(gate_val) * up_val).astype(jnp.bfloat16)
    ffn_total = lax.psum(
        jnp.dot(hidden_ff, down_weight, preferred_element_type=jnp.float32).astype(jnp.bfloat16),
        "tp",
    ).astype(jnp.float32)
    result = (middle + ffn_total).astype(jnp.bfloat16)
    return (result.reshape(prompt_batch, sequence_length, model_width), kv_cache)


def solution(mesh):
    placed = (
        P("req", None, None),
        P("req"),
        P(),
        P(),
        P(("req", "tp"), None),
        P(("req", "tp"), None),
        P(("req", "tp"), None),
        P(("req", "tp"), None),
        P(("req", "tp"), None),
        P(("req", "tp"), None),
        P(("req", "tp"), None),
    )
    return jax.shard_map(
        local,
        mesh=mesh,
        in_specs=placed,
        out_specs=(P("req", None, None), P("req", None, None)),
        check_vma=False,
    )
```

```python
import math

import jax
import jax.numpy as jnp
from jax import lax
from jax.sharding import PartitionSpec as P

QUERY_HEADS = 20
KEY_VALUE_HEADS = 5
HEAD_DIM = 64


def rms_norm(field, gain_vec):
    scale = lax.rsqrt(jnp.mean(field * field, axis=-1, keepdims=True) + 1e-05)
    return (field * scale * gain_vec).astype(jnp.bfloat16)


def rope_tables(sequence_length, head_size):
    half_width = head_size // 2
    positions = jnp.arange(sequence_length, dtype=jnp.float32)[:, None]
    frequency = jnp.exp(
        -math.log(10000.0) * (2.0 * jnp.arange(half_width, dtype=jnp.float32) / head_size)
    )
    angles = positions * frequency[None, :]
    return (jnp.cos(angles), jnp.sin(angles))


def rotate(field, cosine_table, sine_table):
    half_width = field.shape[-1] // 2
    first_half = field[..., :half_width]
    second_half = field[..., half_width:]
    cos_b = cosine_table[:, None, :]
    sin_b = sine_table[:, None, :]
    return jnp.concatenate(
        [first_half * cos_b - second_half * sin_b, second_half * cos_b + first_half * sin_b],
        axis=-1,
    )


CHIP_PAIRS = [(0, 1), (1, 0), (2, 3), (3, 2)]
CROSS_PAIRS = [(0, 2), (2, 0), (1, 3), (3, 1)]


def pick(stack, index):
    return lax.dynamic_index_in_dim(stack, index, axis=0, keepdims=False)


def tp_reduce_scatter(partial, core_bit, chip_bit):
    rows, width = partial.shape
    halves = partial.reshape(2, rows // 2, width)
    got = lax.ppermute(pick(halves, 1 - core_bit), "tp", CHIP_PAIRS)
    first = pick(halves, core_bit).astype(jnp.float32) + got.astype(jnp.float32)
    quarters = first.reshape(2, rows // 4, width)
    sent = pick(quarters, 1 - chip_bit).astype(jnp.bfloat16)
    got = lax.ppermute(sent, "tp", CROSS_PAIRS)
    return pick(quarters, chip_bit) + got.astype(jnp.float32)


def tp_all_gather(quarter, core_bit, chip_bit):
    got = lax.ppermute(quarter, "tp", CROSS_PAIRS)
    half = jnp.where(
        chip_bit == 0,
        jnp.concatenate([quarter, got], axis=0),
        jnp.concatenate([got, quarter], axis=0),
    )
    got = lax.ppermute(half, "tp", CHIP_PAIRS)
    return jnp.where(
        core_bit == 0,
        jnp.concatenate([half, got], axis=0),
        jnp.concatenate([got, half], axis=0),
    )


def local(
    hidden_in,
    lengths,
    attn_gain,
    mlp_gain,
    q_master,
    k_master,
    trainer_value_weight,
    o_master,
    gate_master,
    up_master,
    down_master,
):
    tp_count = lax.axis_size("tp")
    req_count = lax.axis_size("req")
    tensor_shard_index = lax.axis_index("tp")
    core_bit = tensor_shard_index % 2
    chip_bit = tensor_shard_index // 2
    bf = jnp.bfloat16
    q_cols = q_master.shape[1] // tp_count
    kv_cols = k_master.shape[1]
    ff_cols = gate_master.shape[1] // tp_count
    local_rows = q_master.shape[0]
    model_cols = o_master.shape[1]
    block_rows = tp_count * local_rows

    def dest_chunk(dest):
        return jnp.concatenate(
            [
                q_master[:, dest * q_cols : (dest + 1) * q_cols],
                k_master,
                trainer_value_weight,
                gate_master[:, dest * ff_cols : (dest + 1) * ff_cols],
                up_master[:, dest * ff_cols : (dest + 1) * ff_cols],
            ],
            axis=1,
        ).astype(bf)

    send = jnp.stack([dest_chunk(d) for d in range(tp_count)])
    recv = lax.all_to_all(send, "tp", 0, 0, tiled=False)
    col_block = recv.reshape(block_rows, -1)
    qkv_width = q_cols + 2 * kv_cols

    o_size = o_master.size
    row_pack = jnp.concatenate([o_master.reshape(-1), down_master.reshape(-1)]).astype(bf)
    per_block = req_count // tp_count
    perm = []
    for r_src in range(req_count):
        for t_src in range(tp_count):
            r_dst = tp_count * (r_src % per_block) + t_src
            t_dst = r_src // per_block
            perm.append((r_src * tp_count + t_src, r_dst * tp_count + t_dst))
    row_pack = lax.ppermute(row_pack, ("req", "tp"), perm)

    attn_pack = jnp.concatenate(
        [col_block[:, :qkv_width], row_pack[:o_size].reshape(block_rows, -1)], axis=1
    )
    ffn_pack = jnp.concatenate(
        [col_block[:, qkv_width:], row_pack[o_size:].reshape(block_rows, -1)], axis=1
    )
    attn_all = lax.all_gather(attn_pack, "req", axis=0, tiled=True)
    ffn_all = lax.all_gather(ffn_pack, "req", axis=0, tiled=True)
    qkv_weight = attn_all[:, :qkv_width]
    out_weight = attn_all[:, qkv_width:].reshape(req_count, -1).reshape(-1, model_cols)
    gate_up_weight = ffn_all[:, : 2 * ff_cols]
    down_weight = ffn_all[:, 2 * ff_cols :].reshape(req_count, -1).reshape(-1, model_cols)

    prompt_batch, sequence_length, model_width = hidden_in.shape
    tok_rows = prompt_batch * sequence_length
    flat_rows = hidden_in.reshape(tok_rows, model_width).astype(jnp.float32)
    normalized_input = rms_norm(flat_rows, attn_gain)
    local_heads = q_cols // HEAD_DIM
    qkv = jnp.dot(normalized_input, qkv_weight, preferred_element_type=jnp.float32)
    queries = qkv[:, :q_cols].reshape(prompt_batch, sequence_length, local_heads, HEAD_DIM)
    key_rows = qkv[:, q_cols : q_cols + kv_cols].reshape(
        prompt_batch, sequence_length, KEY_VALUE_HEADS, HEAD_DIM
    )
    value_rows = qkv[:, q_cols + kv_cols :].reshape(
        prompt_batch, sequence_length, KEY_VALUE_HEADS, HEAD_DIM
    )
    cosine_table, sine_table = rope_tables(sequence_length, HEAD_DIM)
    q_rot = rotate(queries, cosine_table, sine_table).astype(jnp.bfloat16)
    rotated_keys = rotate(key_rows, cosine_table, sine_table).astype(jnp.bfloat16)
    value_halves = value_rows.astype(jnp.bfloat16)
    kv_cache = jnp.concatenate(
        [
            rotated_keys.reshape(prompt_batch, sequence_length, KEY_VALUE_HEADS * HEAD_DIM),
            value_halves.reshape(prompt_batch, sequence_length, KEY_VALUE_HEADS * HEAD_DIM),
        ],
        axis=2,
    )
    owner_shards = (
        tensor_shard_index * local_heads + jnp.arange(local_heads, dtype=jnp.int32)
    ) // (QUERY_HEADS // KEY_VALUE_HEADS)
    selector_mask = (
        owner_shards[:, None] == jnp.arange(KEY_VALUE_HEADS, dtype=jnp.int32)[None, :]
    ).astype(jnp.bfloat16)
    k_local = jnp.einsum(
        "pshd,gh->psgd", rotated_keys, selector_mask, preferred_element_type=jnp.float32
    ).astype(jnp.bfloat16)
    v_local = jnp.einsum(
        "pshd,gh->psgd", value_halves, selector_mask, preferred_element_type=jnp.float32
    ).astype(jnp.bfloat16)
    scores = jnp.einsum(
        "pqhd,pkhd->phqk", q_rot, k_local, preferred_element_type=jnp.float32
    ) / math.sqrt(HEAD_DIM)
    row_index = jnp.arange(sequence_length, dtype=jnp.int32)[:, None]
    col_index = jnp.arange(sequence_length, dtype=jnp.int32)[None, :]
    allowed = (col_index <= row_index)[None, None] & (
        col_index[None, None] < lengths[:, None, None, None]
    )
    scores = jnp.where(allowed, scores, -1e30)
    highest = jnp.max(scores, axis=-1, keepdims=True)
    expo = jnp.exp(scores - highest)
    weight_table = (expo / jnp.sum(expo, axis=-1, keepdims=True)).astype(jnp.bfloat16)
    attended = (
        jnp.einsum("phqk,pkhd->pqhd", weight_table, v_local, preferred_element_type=jnp.float32)
        .astype(jnp.bfloat16)
        .reshape(tok_rows, local_heads * HEAD_DIM)
    )
    attn_partial = jnp.dot(attended, out_weight, preferred_element_type=jnp.float32).astype(bf)
    attn_mine = tp_reduce_scatter(attn_partial, core_bit, chip_bit)
    quarter_rows = tok_rows // tp_count
    row_start = (core_bit * 2 + chip_bit) * quarter_rows
    middle = lax.dynamic_slice_in_dim(flat_rows, row_start, quarter_rows, 0) + attn_mine
    normed_mine = rms_norm(middle, mlp_gain)
    normed_rows = tp_all_gather(normed_mine, core_bit, chip_bit)
    gate_up = jnp.dot(normed_rows, gate_up_weight, preferred_element_type=jnp.float32)
    gate_val = gate_up[:, :ff_cols]
    up_val = gate_up[:, ff_cols:]
    hidden_ff = (jax.nn.silu(gate_val) * up_val).astype(jnp.bfloat16)
    ffn_partial = jnp.dot(hidden_ff, down_weight, preferred_element_type=jnp.float32).astype(bf)
    ffn_mine = tp_reduce_scatter(ffn_partial, core_bit, chip_bit)
    result_mine = (middle + ffn_mine).astype(jnp.bfloat16)
    result = tp_all_gather(result_mine, core_bit, chip_bit)
    return (result.reshape(prompt_batch, sequence_length, model_width), kv_cache)


def solution(mesh):
    placed = (
        P("req", None, None),
        P("req"),
        P(),
        P(),
        P(("req", "tp"), None),
        P(("req", "tp"), None),
        P(("req", "tp"), None),
        P(("req", "tp"), None),
        P(("req", "tp"), None),
        P(("req", "tp"), None),
        P(("req", "tp"), None),
    )
    return jax.shard_map(
        local,
        mesh=mesh,
        in_specs=placed,
        out_specs=(P("req", None, None), P("req", None, None)),
        check_vma=False,
    )
```

```python
import math

import jax
import jax.numpy as jnp
from jax import lax
from jax.sharding import PartitionSpec as P

QUERY_HEADS = 20
KEY_VALUE_HEADS = 5
HEAD_DIM = 64


def rms_norm(field, gain_vec):
    scale = lax.rsqrt(jnp.mean(field * field, axis=-1, keepdims=True) + 1e-05)
    return (field * scale * gain_vec).astype(jnp.bfloat16)


def rope_tables(sequence_length, head_size):
    half_width = head_size // 2
    positions = jnp.arange(sequence_length, dtype=jnp.float32)[:, None]
    frequency = jnp.exp(
        -math.log(10000.0) * (2.0 * jnp.arange(half_width, dtype=jnp.float32) / head_size)
    )
    angles = positions * frequency[None, :]
    return (jnp.cos(angles), jnp.sin(angles))


def rotate(field, cosine_table, sine_table):
    half_width = field.shape[-1] // 2
    first_half = field[..., :half_width]
    second_half = field[..., half_width:]
    cos_b = cosine_table[:, None, :]
    sin_b = sine_table[:, None, :]
    return jnp.concatenate(
        [first_half * cos_b - second_half * sin_b, second_half * cos_b + first_half * sin_b],
        axis=-1,
    )


REQ_DIMS = (4, 4, 2)
CHIP_PAIRS = [(0, 1), (1, 0), (2, 3), (3, 2)]
CROSS_PAIRS = [(0, 2), (2, 0), (1, 3), (3, 1)]


def pick(stack, index):
    return lax.dynamic_index_in_dim(stack, index, axis=0, keepdims=False)


def tp_reduce_scatter(partial, core_bit, chip_bit):
    rows, width = partial.shape
    halves = partial.reshape(2, rows // 2, width)
    got = lax.ppermute(pick(halves, 1 - core_bit), "tp", CHIP_PAIRS)
    first = pick(halves, core_bit).astype(jnp.float32) + got.astype(jnp.float32)
    quarters = first.reshape(2, rows // 4, width)
    sent = pick(quarters, 1 - chip_bit).astype(jnp.bfloat16)
    got = lax.ppermute(sent, "tp", CROSS_PAIRS)
    return pick(quarters, chip_bit) + got.astype(jnp.float32)


def tp_all_gather(quarter, core_bit, chip_bit):
    got = lax.ppermute(quarter, "tp", CROSS_PAIRS)
    half = jnp.where(
        chip_bit == 0,
        jnp.concatenate([quarter, got], axis=0),
        jnp.concatenate([got, quarter], axis=0),
    )
    got = lax.ppermute(half, "tp", CHIP_PAIRS)
    return jnp.where(
        core_bit == 0,
        jnp.concatenate([half, got], axis=0),
        jnp.concatenate([got, half], axis=0),
    )


def ring_step(block, pos, size, shift_pairs):
    up, down = shift_pairs
    buf = jnp.zeros((size,) + block.shape, block.dtype)
    buf = lax.dynamic_update_index_in_dim(buf, block, pos, 0)
    from_below = lax.ppermute(block, "req", up)
    from_above = lax.ppermute(block, "req", down)
    buf = lax.dynamic_update_index_in_dim(buf, from_below, (pos + size - 1) % size, 0)
    buf = lax.dynamic_update_index_in_dim(buf, from_above, (pos + 1) % size, 0)
    half = block.shape[0] // 2
    far_low = lax.ppermute(from_below[:half], "req", up)
    far_high = lax.ppermute(from_above[half:], "req", down)
    far = jnp.concatenate([far_low, far_high], axis=0)
    buf = lax.dynamic_update_index_in_dim(buf, far, (pos + 2) % size, 0)
    return buf.reshape((size * block.shape[0],) + block.shape[1:])


def req_all_gather(block, req_index, dims):
    nz, nx, ny = dims
    z = req_index // (nx * ny)
    x = (req_index // ny) % nx
    y = req_index % ny
    ids = [(a, b, c) for a in range(nz) for b in range(nx) for c in range(ny)]

    def lin(a, b, c):
        return (a * nx + b) * ny + c

    got = lax.ppermute(block, "req", [(lin(a, b, c), lin(a, b, 1 - c)) for a, b, c in ids])
    pair = jnp.where(y == 0, jnp.concatenate([block, got], 0), jnp.concatenate([got, block], 0))
    x_pairs = (
        [(lin(a, b, c), lin(a, (b + 1) % nx, c)) for a, b, c in ids],
        [(lin(a, b, c), lin(a, (b - 1) % nx, c)) for a, b, c in ids],
    )
    row = ring_step(pair, x, nx, x_pairs)
    z_pairs = (
        [(lin(a, b, c), lin((a + 1) % nz, b, c)) for a, b, c in ids],
        [(lin(a, b, c), lin((a - 1) % nz, b, c)) for a, b, c in ids],
    )
    return ring_step(row, z, nz, z_pairs)


def local(
    hidden_in,
    lengths,
    attn_gain,
    mlp_gain,
    q_master,
    k_master,
    trainer_value_weight,
    o_master,
    gate_master,
    up_master,
    down_master,
):
    tp_count = lax.axis_size("tp")
    req_count = lax.axis_size("req")
    tensor_shard_index = lax.axis_index("tp")
    core_bit = tensor_shard_index % 2
    chip_bit = tensor_shard_index // 2
    bf = jnp.bfloat16
    q_cols = q_master.shape[1] // tp_count
    kv_cols = k_master.shape[1]
    ff_cols = gate_master.shape[1] // tp_count
    local_rows = q_master.shape[0]
    model_cols = o_master.shape[1]
    block_rows = tp_count * local_rows

    def dest_chunk(dest):
        return jnp.concatenate(
            [
                q_master[:, dest * q_cols : (dest + 1) * q_cols],
                k_master,
                trainer_value_weight,
                gate_master[:, dest * ff_cols : (dest + 1) * ff_cols],
                up_master[:, dest * ff_cols : (dest + 1) * ff_cols],
            ],
            axis=1,
        ).astype(bf)

    send = jnp.stack([dest_chunk(d) for d in range(tp_count)])
    recv = lax.all_to_all(send, "tp", 0, 0, tiled=False)
    col_block = recv.reshape(block_rows, -1)
    qkv_width = q_cols + 2 * kv_cols

    o_size = o_master.size
    row_pack = jnp.concatenate([o_master.reshape(-1), down_master.reshape(-1)]).astype(bf)
    per_block = req_count // tp_count
    perm = []
    for r_src in range(req_count):
        for t_src in range(tp_count):
            r_dst = tp_count * (r_src % per_block) + t_src
            t_dst = r_src // per_block
            perm.append((r_src * tp_count + t_src, r_dst * tp_count + t_dst))
    row_pack = lax.ppermute(row_pack, ("req", "tp"), perm)

    attn_pack = jnp.concatenate(
        [col_block[:, :qkv_width], row_pack[:o_size].reshape(block_rows, -1)], axis=1
    )
    ffn_pack = jnp.concatenate(
        [col_block[:, qkv_width:], row_pack[o_size:].reshape(block_rows, -1)], axis=1
    )
    req_index = lax.axis_index("req")
    attn_all = req_all_gather(attn_pack, req_index, REQ_DIMS)
    ffn_all = req_all_gather(ffn_pack, req_index, REQ_DIMS)
    qkv_weight = attn_all[:, :qkv_width]
    out_weight = attn_all[:, qkv_width:].reshape(req_count, -1).reshape(-1, model_cols)
    gate_up_weight = ffn_all[:, : 2 * ff_cols]
    down_weight = ffn_all[:, 2 * ff_cols :].reshape(req_count, -1).reshape(-1, model_cols)

    prompt_batch, sequence_length, model_width = hidden_in.shape
    tok_rows = prompt_batch * sequence_length
    flat_rows = hidden_in.reshape(tok_rows, model_width).astype(jnp.float32)
    normalized_input = rms_norm(flat_rows, attn_gain)
    local_heads = q_cols // HEAD_DIM
    qkv = jnp.dot(normalized_input, qkv_weight, preferred_element_type=jnp.float32)
    queries = qkv[:, :q_cols].reshape(prompt_batch, sequence_length, local_heads, HEAD_DIM)
    key_rows = qkv[:, q_cols : q_cols + kv_cols].reshape(
        prompt_batch, sequence_length, KEY_VALUE_HEADS, HEAD_DIM
    )
    value_rows = qkv[:, q_cols + kv_cols :].reshape(
        prompt_batch, sequence_length, KEY_VALUE_HEADS, HEAD_DIM
    )
    cosine_table, sine_table = rope_tables(sequence_length, HEAD_DIM)
    q_rot = rotate(queries, cosine_table, sine_table).astype(jnp.bfloat16)
    rotated_keys = rotate(key_rows, cosine_table, sine_table).astype(jnp.bfloat16)
    value_halves = value_rows.astype(jnp.bfloat16)
    kv_cache = jnp.concatenate(
        [
            rotated_keys.reshape(prompt_batch, sequence_length, KEY_VALUE_HEADS * HEAD_DIM),
            value_halves.reshape(prompt_batch, sequence_length, KEY_VALUE_HEADS * HEAD_DIM),
        ],
        axis=2,
    )
    owner_shards = (
        tensor_shard_index * local_heads + jnp.arange(local_heads, dtype=jnp.int32)
    ) // (QUERY_HEADS // KEY_VALUE_HEADS)
    selector_mask = (
        owner_shards[:, None] == jnp.arange(KEY_VALUE_HEADS, dtype=jnp.int32)[None, :]
    ).astype(jnp.bfloat16)
    k_local = jnp.einsum(
        "pshd,gh->psgd", rotated_keys, selector_mask, preferred_element_type=jnp.float32
    ).astype(jnp.bfloat16)
    v_local = jnp.einsum(
        "pshd,gh->psgd", value_halves, selector_mask, preferred_element_type=jnp.float32
    ).astype(jnp.bfloat16)
    scores = jnp.einsum(
        "pqhd,pkhd->phqk", q_rot, k_local, preferred_element_type=jnp.float32
    ) / math.sqrt(HEAD_DIM)
    row_index = jnp.arange(sequence_length, dtype=jnp.int32)[:, None]
    col_index = jnp.arange(sequence_length, dtype=jnp.int32)[None, :]
    allowed = (col_index <= row_index)[None, None] & (
        col_index[None, None] < lengths[:, None, None, None]
    )
    scores = jnp.where(allowed, scores, -1e30)
    highest = jnp.max(scores, axis=-1, keepdims=True)
    expo = jnp.exp(scores - highest)
    weight_table = (expo / jnp.sum(expo, axis=-1, keepdims=True)).astype(jnp.bfloat16)
    attended = (
        jnp.einsum("phqk,pkhd->pqhd", weight_table, v_local, preferred_element_type=jnp.float32)
        .astype(jnp.bfloat16)
        .reshape(tok_rows, local_heads * HEAD_DIM)
    )
    attn_partial = jnp.dot(attended, out_weight, preferred_element_type=jnp.float32).astype(bf)
    attn_mine = tp_reduce_scatter(attn_partial, core_bit, chip_bit)
    quarter_rows = tok_rows // tp_count
    row_start = (core_bit * 2 + chip_bit) * quarter_rows
    middle = lax.dynamic_slice_in_dim(flat_rows, row_start, quarter_rows, 0) + attn_mine
    normed_mine = rms_norm(middle, mlp_gain)
    normed_rows = tp_all_gather(normed_mine, core_bit, chip_bit)
    gate_up = jnp.dot(normed_rows, gate_up_weight, preferred_element_type=jnp.float32)
    gate_val = gate_up[:, :ff_cols]
    up_val = gate_up[:, ff_cols:]
    hidden_ff = (jax.nn.silu(gate_val) * up_val).astype(jnp.bfloat16)
    ffn_partial = jnp.dot(hidden_ff, down_weight, preferred_element_type=jnp.float32).astype(bf)
    ffn_mine = tp_reduce_scatter(ffn_partial, core_bit, chip_bit)
    result_mine = (middle + ffn_mine).astype(jnp.bfloat16)
    result = tp_all_gather(result_mine, core_bit, chip_bit)
    return (result.reshape(prompt_batch, sequence_length, model_width), kv_cache)


def solution(mesh):
    placed = (
        P("req", None, None),
        P("req"),
        P(),
        P(),
        P(("req", "tp"), None),
        P(("req", "tp"), None),
        P(("req", "tp"), None),
        P(("req", "tp"), None),
        P(("req", "tp"), None),
        P(("req", "tp"), None),
        P(("req", "tp"), None),
    )
    return jax.shard_map(
        local,
        mesh=mesh,
        in_specs=placed,
        out_specs=(P("req", None, None), P("req", None, None)),
        check_vma=False,
    )
```

```python
import math

import jax
import jax.numpy as jnp
from jax import lax
from jax.sharding import PartitionSpec as P

QUERY_HEADS = 20
KEY_VALUE_HEADS = 5
HEAD_DIM = 64


def rms_norm(field, gain_vec):
    scale = lax.rsqrt(jnp.mean(field * field, axis=-1, keepdims=True) + 1e-05)
    return (field * scale * gain_vec).astype(jnp.bfloat16)


def rope_tables(sequence_length, head_size):
    half_width = head_size // 2
    positions = jnp.arange(sequence_length, dtype=jnp.float32)[:, None]
    frequency = jnp.exp(
        -math.log(10000.0) * (2.0 * jnp.arange(half_width, dtype=jnp.float32) / head_size)
    )
    angles = positions * frequency[None, :]
    return (jnp.cos(angles), jnp.sin(angles))


def rotate(field, cosine_table, sine_table):
    half_width = field.shape[-1] // 2
    first_half = field[..., :half_width]
    second_half = field[..., half_width:]
    cos_b = cosine_table[:, None, :]
    sin_b = sine_table[:, None, :]
    return jnp.concatenate(
        [first_half * cos_b - second_half * sin_b, second_half * cos_b + first_half * sin_b],
        axis=-1,
    )


REQ_DIMS = (4, 4, 2)
CHIP_PAIRS = [(0, 1), (1, 0), (2, 3), (3, 2)]
CROSS_PAIRS = [(0, 2), (2, 0), (1, 3), (3, 1)]


def pick(stack, index):
    return lax.dynamic_index_in_dim(stack, index, axis=0, keepdims=False)


def tp_reduce_scatter(partial, core_bit, chip_bit):
    rows, width = partial.shape
    halves = partial.reshape(2, rows // 2, width)
    got = lax.ppermute(pick(halves, 1 - core_bit), "tp", CHIP_PAIRS)
    first = pick(halves, core_bit).astype(jnp.float32) + got.astype(jnp.float32)
    quarters = first.reshape(2, rows // 4, width)
    sent = pick(quarters, 1 - chip_bit).astype(jnp.bfloat16)
    got = lax.ppermute(sent, "tp", CROSS_PAIRS)
    return pick(quarters, chip_bit) + got.astype(jnp.float32)


def tp_all_gather(quarter, core_bit, chip_bit):
    got = lax.ppermute(quarter, "tp", CROSS_PAIRS)
    half = jnp.where(
        chip_bit == 0,
        jnp.concatenate([quarter, got], axis=0),
        jnp.concatenate([got, quarter], axis=0),
    )
    got = lax.ppermute(half, "tp", CHIP_PAIRS)
    return jnp.where(
        core_bit == 0,
        jnp.concatenate([half, got], axis=0),
        jnp.concatenate([got, half], axis=0),
    )


def ring_step(block, pos, size, shift_pairs):
    up, down = shift_pairs
    buf = jnp.zeros((size,) + block.shape, block.dtype)
    buf = lax.dynamic_update_index_in_dim(buf, block, pos, 0)
    from_below = lax.ppermute(block, "req", up)
    from_above = lax.ppermute(block, "req", down)
    buf = lax.dynamic_update_index_in_dim(buf, from_below, (pos + size - 1) % size, 0)
    buf = lax.dynamic_update_index_in_dim(buf, from_above, (pos + 1) % size, 0)
    half = block.shape[0] // 2
    far_low = lax.ppermute(from_below[:half], "req", up)
    far_high = lax.ppermute(from_above[half:], "req", down)
    far = jnp.concatenate([far_low, far_high], axis=0)
    buf = lax.dynamic_update_index_in_dim(buf, far, (pos + 2) % size, 0)
    return buf.reshape((size * block.shape[0],) + block.shape[1:])


def req_gather_stages(req_index, dims):
    nz, nx, ny = dims
    z = req_index // (nx * ny)
    x = (req_index // ny) % nx
    y = req_index % ny
    ids = [(a, b, c) for a in range(nz) for b in range(nx) for c in range(ny)]

    def lin(a, b, c):
        return (a * nx + b) * ny + c

    y_pairs = [(lin(a, b, c), lin(a, b, 1 - c)) for a, b, c in ids]
    x_pairs = (
        [(lin(a, b, c), lin(a, (b + 1) % nx, c)) for a, b, c in ids],
        [(lin(a, b, c), lin(a, (b - 1) % nx, c)) for a, b, c in ids],
    )
    z_pairs = (
        [(lin(a, b, c), lin((a + 1) % nz, b, c)) for a, b, c in ids],
        [(lin(a, b, c), lin((a - 1) % nz, b, c)) for a, b, c in ids],
    )

    def y_stage(block):
        got = lax.ppermute(block, "req", y_pairs)
        return jnp.where(
            y == 0, jnp.concatenate([block, got], 0), jnp.concatenate([got, block], 0)
        )

    def x_stage(block):
        return ring_step(block, x, nx, x_pairs)

    def z_stage(block):
        return ring_step(block, z, nz, z_pairs)

    return y_stage, x_stage, z_stage


def local(
    hidden_in,
    lengths,
    attn_gain,
    mlp_gain,
    q_master,
    k_master,
    trainer_value_weight,
    o_master,
    gate_master,
    up_master,
    down_master,
):
    tp_count = lax.axis_size("tp")
    req_count = lax.axis_size("req")
    tensor_shard_index = lax.axis_index("tp")
    core_bit = tensor_shard_index % 2
    chip_bit = tensor_shard_index // 2
    bf = jnp.bfloat16
    q_cols = q_master.shape[1] // tp_count
    kv_cols = k_master.shape[1]
    ff_cols = gate_master.shape[1] // tp_count
    local_rows = q_master.shape[0]
    model_cols = o_master.shape[1]
    block_rows = tp_count * local_rows

    def dest_chunk(dest):
        return jnp.concatenate(
            [
                q_master[:, dest * q_cols : (dest + 1) * q_cols],
                k_master,
                trainer_value_weight,
                gate_master[:, dest * ff_cols : (dest + 1) * ff_cols],
                up_master[:, dest * ff_cols : (dest + 1) * ff_cols],
            ],
            axis=1,
        ).astype(bf)

    send = jnp.stack([dest_chunk(d) for d in range(tp_count)])
    recv = lax.all_to_all(send, "tp", 0, 0, tiled=False)
    col_block = recv.reshape(block_rows, -1)
    qkv_width = q_cols + 2 * kv_cols

    o_size = o_master.size
    row_pack = jnp.concatenate([o_master.reshape(-1), down_master.reshape(-1)]).astype(bf)
    per_block = req_count // tp_count
    perm = []
    for r_src in range(req_count):
        for t_src in range(tp_count):
            r_dst = tp_count * (r_src % per_block) + t_src
            t_dst = r_src // per_block
            perm.append((r_src * tp_count + t_src, r_dst * tp_count + t_dst))
    row_pack = lax.ppermute(row_pack, ("req", "tp"), perm)

    attn_pack = jnp.concatenate(
        [col_block[:, :qkv_width], row_pack[:o_size].reshape(block_rows, -1)], axis=1
    )
    ffn_pack = jnp.concatenate(
        [col_block[:, qkv_width:], row_pack[o_size:].reshape(block_rows, -1)], axis=1
    )
    y_stage, x_stage, z_stage = req_gather_stages(lax.axis_index("req"), REQ_DIMS)
    attn_y = y_stage(attn_pack)
    ffn_y = y_stage(ffn_pack)
    attn_x = x_stage(attn_y)
    attn_x, ffn_y = lax.optimization_barrier((attn_x, ffn_y))
    ffn_x = x_stage(ffn_y)
    attn_all = z_stage(attn_x)
    attn_all, ffn_x = lax.optimization_barrier((attn_all, ffn_x))
    ffn_all = z_stage(ffn_x)
    qkv_weight = attn_all[:, :qkv_width]
    out_weight = attn_all[:, qkv_width:].reshape(req_count, -1).reshape(-1, model_cols)
    gate_up_weight = ffn_all[:, : 2 * ff_cols]
    down_weight = ffn_all[:, 2 * ff_cols :].reshape(req_count, -1).reshape(-1, model_cols)

    prompt_batch, sequence_length, model_width = hidden_in.shape
    tok_rows = prompt_batch * sequence_length
    flat_rows = hidden_in.reshape(tok_rows, model_width).astype(jnp.float32)
    normalized_input = rms_norm(flat_rows, attn_gain)
    local_heads = q_cols // HEAD_DIM
    qkv = jnp.dot(normalized_input, qkv_weight, preferred_element_type=jnp.float32)
    queries = qkv[:, :q_cols].reshape(prompt_batch, sequence_length, local_heads, HEAD_DIM)
    key_rows = qkv[:, q_cols : q_cols + kv_cols].reshape(
        prompt_batch, sequence_length, KEY_VALUE_HEADS, HEAD_DIM
    )
    value_rows = qkv[:, q_cols + kv_cols :].reshape(
        prompt_batch, sequence_length, KEY_VALUE_HEADS, HEAD_DIM
    )
    cosine_table, sine_table = rope_tables(sequence_length, HEAD_DIM)
    q_rot = rotate(queries, cosine_table, sine_table).astype(jnp.bfloat16)
    rotated_keys = rotate(key_rows, cosine_table, sine_table).astype(jnp.bfloat16)
    value_halves = value_rows.astype(jnp.bfloat16)
    kv_cache = jnp.concatenate(
        [
            rotated_keys.reshape(prompt_batch, sequence_length, KEY_VALUE_HEADS * HEAD_DIM),
            value_halves.reshape(prompt_batch, sequence_length, KEY_VALUE_HEADS * HEAD_DIM),
        ],
        axis=2,
    )
    owner_shards = (
        tensor_shard_index * local_heads + jnp.arange(local_heads, dtype=jnp.int32)
    ) // (QUERY_HEADS // KEY_VALUE_HEADS)
    selector_mask = (
        owner_shards[:, None] == jnp.arange(KEY_VALUE_HEADS, dtype=jnp.int32)[None, :]
    ).astype(jnp.bfloat16)
    k_local = jnp.einsum(
        "pshd,gh->psgd", rotated_keys, selector_mask, preferred_element_type=jnp.float32
    ).astype(jnp.bfloat16)
    v_local = jnp.einsum(
        "pshd,gh->psgd", value_halves, selector_mask, preferred_element_type=jnp.float32
    ).astype(jnp.bfloat16)
    scores = jnp.einsum(
        "pqhd,pkhd->phqk", q_rot, k_local, preferred_element_type=jnp.float32
    ) / math.sqrt(HEAD_DIM)
    row_index = jnp.arange(sequence_length, dtype=jnp.int32)[:, None]
    col_index = jnp.arange(sequence_length, dtype=jnp.int32)[None, :]
    allowed = (col_index <= row_index)[None, None] & (
        col_index[None, None] < lengths[:, None, None, None]
    )
    scores = jnp.where(allowed, scores, -1e30)
    highest = jnp.max(scores, axis=-1, keepdims=True)
    expo = jnp.exp(scores - highest)
    weight_table = (expo / jnp.sum(expo, axis=-1, keepdims=True)).astype(jnp.bfloat16)
    attended = (
        jnp.einsum("phqk,pkhd->pqhd", weight_table, v_local, preferred_element_type=jnp.float32)
        .astype(jnp.bfloat16)
        .reshape(tok_rows, local_heads * HEAD_DIM)
    )
    attended, ffn_all = lax.optimization_barrier((attended, ffn_all))
    attn_partial = jnp.dot(attended, out_weight, preferred_element_type=jnp.float32).astype(bf)
    attn_mine = tp_reduce_scatter(attn_partial, core_bit, chip_bit)
    quarter_rows = tok_rows // tp_count
    row_start = (core_bit * 2 + chip_bit) * quarter_rows
    middle = lax.dynamic_slice_in_dim(flat_rows, row_start, quarter_rows, 0) + attn_mine
    normed_mine = rms_norm(middle, mlp_gain)
    normed_rows = tp_all_gather(normed_mine, core_bit, chip_bit)
    gate_up = jnp.dot(normed_rows, gate_up_weight, preferred_element_type=jnp.float32)
    gate_val = gate_up[:, :ff_cols]
    up_val = gate_up[:, ff_cols:]
    hidden_ff = (jax.nn.silu(gate_val) * up_val).astype(jnp.bfloat16)
    ffn_partial = jnp.dot(hidden_ff, down_weight, preferred_element_type=jnp.float32).astype(bf)
    ffn_mine = tp_reduce_scatter(ffn_partial, core_bit, chip_bit)
    result_mine = (middle + ffn_mine).astype(jnp.bfloat16)
    result = tp_all_gather(result_mine, core_bit, chip_bit)
    return (result.reshape(prompt_batch, sequence_length, model_width), kv_cache)


def solution(mesh):
    placed = (
        P("req", None, None),
        P("req"),
        P(),
        P(),
        P(("req", "tp"), None),
        P(("req", "tp"), None),
        P(("req", "tp"), None),
        P(("req", "tp"), None),
        P(("req", "tp"), None),
        P(("req", "tp"), None),
        P(("req", "tp"), None),
    )
    return jax.shard_map(
        local,
        mesh=mesh,
        in_specs=placed,
        out_specs=(P("req", None, None), P("req", None, None)),
        check_vma=False,
    )
```

```python
import math

import jax
import jax.numpy as jnp
from jax import lax
from jax.sharding import PartitionSpec as P

QUERY_HEADS = 20
KEY_VALUE_HEADS = 5
HEAD_DIM = 64


def rms_norm(field, gain_vec):
    scale = lax.rsqrt(jnp.mean(field * field, axis=-1, keepdims=True) + 1e-05)
    return (field * scale * gain_vec).astype(jnp.bfloat16)


def rope_tables(sequence_length, head_size):
    half_width = head_size // 2
    positions = jnp.arange(sequence_length, dtype=jnp.float32)[:, None]
    frequency = jnp.exp(
        -math.log(10000.0) * (2.0 * jnp.arange(half_width, dtype=jnp.float32) / head_size)
    )
    angles = positions * frequency[None, :]
    return (jnp.cos(angles), jnp.sin(angles))


def rotate(field, cosine_table, sine_table):
    half_width = field.shape[-1] // 2
    first_half = field[..., :half_width]
    second_half = field[..., half_width:]
    cos_b = cosine_table[:, None, :]
    sin_b = sine_table[:, None, :]
    return jnp.concatenate(
        [first_half * cos_b - second_half * sin_b, second_half * cos_b + first_half * sin_b],
        axis=-1,
    )


REQ_DIMS = (4, 4, 2)
CHIP_PAIRS = [(0, 1), (1, 0), (2, 3), (3, 2)]
CROSS_PAIRS = [(0, 2), (2, 0), (1, 3), (3, 1)]


def pick(stack, index):
    return lax.dynamic_index_in_dim(stack, index, axis=0, keepdims=False)


def tp_reduce_scatter(partial, core_bit, chip_bit):
    rows, width = partial.shape
    halves = partial.reshape(2, rows // 2, width)
    got = lax.ppermute(pick(halves, 1 - core_bit), "tp", CHIP_PAIRS)
    first = pick(halves, core_bit).astype(jnp.float32) + got.astype(jnp.float32)
    quarters = first.reshape(2, rows // 4, width)
    sent = pick(quarters, 1 - chip_bit).astype(jnp.bfloat16)
    got = lax.ppermute(sent, "tp", CROSS_PAIRS)
    return pick(quarters, chip_bit) + got.astype(jnp.float32)


def tp_all_gather(quarter, core_bit, chip_bit):
    got = lax.ppermute(quarter, "tp", CROSS_PAIRS)
    half = jnp.zeros((2,) + quarter.shape, quarter.dtype)
    half = lax.dynamic_update_index_in_dim(half, quarter, chip_bit, 0)
    half = lax.dynamic_update_index_in_dim(half, got, 1 - chip_bit, 0)
    half = half.reshape((-1,) + quarter.shape[1:])
    got = lax.ppermute(half, "tp", CHIP_PAIRS)
    full = jnp.zeros((2,) + half.shape, half.dtype)
    full = lax.dynamic_update_index_in_dim(full, half, core_bit, 0)
    full = lax.dynamic_update_index_in_dim(full, got, 1 - core_bit, 0)
    return full.reshape((-1,) + half.shape[1:])


def ring_step(block, pos, size, shift_pairs):
    up, down = shift_pairs
    buf = jnp.zeros((size,) + block.shape, block.dtype)
    buf = lax.dynamic_update_index_in_dim(buf, block, pos, 0)
    from_below = lax.ppermute(block, "req", up)
    from_above = lax.ppermute(block, "req", down)
    buf = lax.dynamic_update_index_in_dim(buf, from_below, (pos + size - 1) % size, 0)
    buf = lax.dynamic_update_index_in_dim(buf, from_above, (pos + 1) % size, 0)
    half = block.shape[0] // 2
    far_low = lax.ppermute(from_below[:half], "req", up)
    far_high = lax.ppermute(from_above[half:], "req", down)
    far = jnp.concatenate([far_low, far_high], axis=0)
    buf = lax.dynamic_update_index_in_dim(buf, far, (pos + 2) % size, 0)
    return buf.reshape((size * block.shape[0],) + block.shape[1:])


def req_gather_stages(req_index, dims):
    nz, nx, ny = dims
    z = req_index // (nx * ny)
    x = (req_index // ny) % nx
    y = req_index % ny
    ids = [(a, b, c) for a in range(nz) for b in range(nx) for c in range(ny)]

    def lin(a, b, c):
        return (a * nx + b) * ny + c

    y_pairs = [(lin(a, b, c), lin(a, b, 1 - c)) for a, b, c in ids]
    x_pairs = (
        [(lin(a, b, c), lin(a, (b + 1) % nx, c)) for a, b, c in ids],
        [(lin(a, b, c), lin(a, (b - 1) % nx, c)) for a, b, c in ids],
    )
    z_pairs = (
        [(lin(a, b, c), lin((a + 1) % nz, b, c)) for a, b, c in ids],
        [(lin(a, b, c), lin((a - 1) % nz, b, c)) for a, b, c in ids],
    )

    def y_stage(block):
        got = lax.ppermute(block, "req", y_pairs)
        return jnp.where(
            y == 0, jnp.concatenate([block, got], 0), jnp.concatenate([got, block], 0)
        )

    def x_stage(block):
        return ring_step(block, x, nx, x_pairs)

    def z_stage(block):
        return ring_step(block, z, nz, z_pairs)

    return y_stage, x_stage, z_stage


def local(
    hidden_in,
    lengths,
    attn_gain,
    mlp_gain,
    q_master,
    k_master,
    trainer_value_weight,
    o_master,
    gate_master,
    up_master,
    down_master,
):
    tp_count = lax.axis_size("tp")
    req_count = lax.axis_size("req")
    tensor_shard_index = lax.axis_index("tp")
    core_bit = tensor_shard_index % 2
    chip_bit = tensor_shard_index // 2
    bf = jnp.bfloat16
    q_cols = q_master.shape[1] // tp_count
    kv_cols = k_master.shape[1]
    ff_cols = gate_master.shape[1] // tp_count
    local_rows = q_master.shape[0]
    model_cols = o_master.shape[1]
    block_rows = tp_count * local_rows

    def dest_chunk(dest):
        return jnp.concatenate(
            [
                q_master[:, dest * q_cols : (dest + 1) * q_cols],
                k_master,
                trainer_value_weight,
                gate_master[:, dest * ff_cols : (dest + 1) * ff_cols],
                up_master[:, dest * ff_cols : (dest + 1) * ff_cols],
            ],
            axis=1,
        ).astype(bf)

    send = jnp.stack([dest_chunk(d) for d in range(tp_count)])
    recv = lax.all_to_all(send, "tp", 0, 0, tiled=False)
    col_block = recv.reshape(block_rows, -1)
    qkv_width = q_cols + 2 * kv_cols

    o_size = o_master.size
    row_pack = jnp.concatenate([o_master.reshape(-1), down_master.reshape(-1)]).astype(bf)
    per_block = req_count // tp_count
    perm = []
    for r_src in range(req_count):
        for t_src in range(tp_count):
            r_dst = tp_count * (r_src % per_block) + t_src
            t_dst = r_src // per_block
            perm.append((r_src * tp_count + t_src, r_dst * tp_count + t_dst))
    row_pack = lax.ppermute(row_pack, ("req", "tp"), perm)

    attn_pack = jnp.concatenate(
        [col_block[:, :qkv_width], row_pack[:o_size].reshape(block_rows, -1)], axis=1
    )
    ffn_pack = jnp.concatenate(
        [col_block[:, qkv_width:], row_pack[o_size:].reshape(block_rows, -1)], axis=1
    )
    y_stage, x_stage, z_stage = req_gather_stages(lax.axis_index("req"), REQ_DIMS)
    attn_y = y_stage(attn_pack)
    ffn_y = y_stage(ffn_pack)
    attn_x = x_stage(attn_y)
    attn_x, ffn_y = lax.optimization_barrier((attn_x, ffn_y))
    ffn_x = x_stage(ffn_y)
    attn_all = z_stage(attn_x)
    attn_all, ffn_x = lax.optimization_barrier((attn_all, ffn_x))
    ffn_all = z_stage(ffn_x)
    qkv_weight = attn_all[:, :qkv_width]
    out_weight = attn_all[:, qkv_width:].reshape(req_count, -1).reshape(-1, model_cols)

    prompt_batch, sequence_length, model_width = hidden_in.shape
    local_heads = q_cols // HEAD_DIM
    cosine_table, sine_table = rope_tables(sequence_length, HEAD_DIM)
    owner_shards = (
        tensor_shard_index * local_heads + jnp.arange(local_heads, dtype=jnp.int32)
    ) // (QUERY_HEADS // KEY_VALUE_HEADS)
    selector_mask = (
        owner_shards[:, None] == jnp.arange(KEY_VALUE_HEADS, dtype=jnp.int32)[None, :]
    ).astype(jnp.bfloat16)
    row_index = jnp.arange(sequence_length, dtype=jnp.int32)[:, None]
    col_index = jnp.arange(sequence_length, dtype=jnp.int32)[None, :]
    quarter_rows = sequence_length // tp_count
    row_start = (core_bit * 2 + chip_bit) * quarter_rows

    def attention(prompt_rows, length):
        flat_rows = prompt_rows.astype(jnp.float32)
        normalized_input = rms_norm(flat_rows, attn_gain)
        qkv = jnp.dot(normalized_input, qkv_weight, preferred_element_type=jnp.float32)
        queries = qkv[:, :q_cols].reshape(sequence_length, local_heads, HEAD_DIM)
        key_rows = qkv[:, q_cols : q_cols + kv_cols].reshape(
            sequence_length, KEY_VALUE_HEADS, HEAD_DIM
        )
        value_rows = qkv[:, q_cols + kv_cols :].reshape(sequence_length, KEY_VALUE_HEADS, HEAD_DIM)
        q_rot = rotate(queries, cosine_table, sine_table).astype(jnp.bfloat16)
        rotated_keys = rotate(key_rows, cosine_table, sine_table).astype(jnp.bfloat16)
        value_halves = value_rows.astype(jnp.bfloat16)
        cache = jnp.concatenate(
            [
                rotated_keys.reshape(sequence_length, KEY_VALUE_HEADS * HEAD_DIM),
                value_halves.reshape(sequence_length, KEY_VALUE_HEADS * HEAD_DIM),
            ],
            axis=1,
        )
        k_local = jnp.einsum(
            "shd,gh->sgd", rotated_keys, selector_mask, preferred_element_type=jnp.float32
        ).astype(jnp.bfloat16)
        v_local = jnp.einsum(
            "shd,gh->sgd", value_halves, selector_mask, preferred_element_type=jnp.float32
        ).astype(jnp.bfloat16)
        scores = jnp.einsum(
            "qhd,khd->hqk", q_rot, k_local, preferred_element_type=jnp.float32
        ) / math.sqrt(HEAD_DIM)
        allowed = (col_index <= row_index)[None] & (col_index[None] < length)
        scores = jnp.where(allowed, scores, -1e30)
        highest = jnp.max(scores, axis=-1, keepdims=True)
        expo = jnp.exp(scores - highest)
        weight_table = (expo / jnp.sum(expo, axis=-1, keepdims=True)).astype(jnp.bfloat16)
        attended = (
            jnp.einsum("hqk,khd->qhd", weight_table, v_local, preferred_element_type=jnp.float32)
            .astype(jnp.bfloat16)
            .reshape(sequence_length, local_heads * HEAD_DIM)
        )
        return flat_rows, attended, cache

    def finish(flat_rows, attended, gate_up_weight, down_weight):
        attn_partial = jnp.dot(attended, out_weight, preferred_element_type=jnp.float32).astype(bf)
        attn_mine = tp_reduce_scatter(attn_partial, core_bit, chip_bit)
        middle = lax.dynamic_slice_in_dim(flat_rows, row_start, quarter_rows, 0) + attn_mine
        normed_mine = rms_norm(middle, mlp_gain)
        normed_rows = tp_all_gather(normed_mine, core_bit, chip_bit)
        gate_up = jnp.dot(normed_rows, gate_up_weight, preferred_element_type=jnp.float32)
        gate_val = gate_up[:, :ff_cols]
        up_val = gate_up[:, ff_cols:]
        hidden_ff = (jax.nn.silu(gate_val) * up_val).astype(jnp.bfloat16)
        ffn_partial = jnp.dot(hidden_ff, down_weight, preferred_element_type=jnp.float32).astype(bf)
        ffn_mine = tp_reduce_scatter(ffn_partial, core_bit, chip_bit)
        result_mine = (middle + ffn_mine).astype(jnp.bfloat16)
        return tp_all_gather(result_mine, core_bit, chip_bit)

    firsts = [attention(hidden_in[p], lengths[p]) for p in range(prompt_batch)]
    first_attended, ffn_all = lax.optimization_barrier((firsts[0][1], ffn_all))
    gate_up_weight = ffn_all[:, : 2 * ff_cols]
    down_weight = ffn_all[:, 2 * ff_cols :].reshape(req_count, -1).reshape(-1, model_cols)
    results = []
    for p, (flat_rows, attended, _) in enumerate(firsts):
        if p == 0:
            attended = first_attended
        results.append(finish(flat_rows, attended, gate_up_weight, down_weight))
    hidden_out = jnp.stack(results)
    kv_cache = jnp.stack([cache for _, _, cache in firsts])
    return (hidden_out, kv_cache)


def solution(mesh):
    placed = (
        P("req", None, None),
        P("req"),
        P(),
        P(),
        P(("req", "tp"), None),
        P(("req", "tp"), None),
        P(("req", "tp"), None),
        P(("req", "tp"), None),
        P(("req", "tp"), None),
        P(("req", "tp"), None),
        P(("req", "tp"), None),
    )
    return jax.shard_map(
        local,
        mesh=mesh,
        in_specs=placed,
        out_specs=(P("req", None, None), P("req", None, None)),
        check_vma=False,
    )
```

```python
import math

import jax
import jax.numpy as jnp
from jax import lax
from jax.experimental import pallas as pl
from jax.experimental.pallas import tpu as pltpu
from jax.sharding import PartitionSpec as P

QUERY_HEADS = 20
KEY_VALUE_HEADS = 5
HEAD_DIM = 64


def rms_norm(field, gain_vec):
    scale = lax.rsqrt(jnp.mean(field * field, axis=-1, keepdims=True) + 1e-05)
    return (field * scale * gain_vec).astype(jnp.bfloat16)


def rope_tables(sequence_length, head_size):
    half_width = head_size // 2
    positions = jnp.arange(sequence_length, dtype=jnp.float32)[:, None]
    frequency = jnp.exp(
        -math.log(10000.0) * (2.0 * jnp.arange(half_width, dtype=jnp.float32) / head_size)
    )
    angles = positions * frequency[None, :]
    return (jnp.cos(angles), jnp.sin(angles))


def rotate(field, cosine_table, sine_table):
    half_width = field.shape[-1] // 2
    first_half = field[..., :half_width]
    second_half = field[..., half_width:]
    cos_b = cosine_table[:, None, :]
    sin_b = sine_table[:, None, :]
    return jnp.concatenate(
        [first_half * cos_b - second_half * sin_b, second_half * cos_b + first_half * sin_b],
        axis=-1,
    )


REQ_DIMS = (4, 4, 2)
CHIP_PAIRS = [(0, 1), (1, 0), (2, 3), (3, 2)]
CROSS_PAIRS = [(0, 2), (2, 0), (1, 3), (3, 1)]


def _attn_body(kv_ref, len_ref, q_ref, k_ref, v_ref, o_ref):
    q = q_ref[0]
    k = k_ref[0]
    v = v_ref[0]
    s = lax.dot_general(q, k, (((1,), (1,)), ((), ())), preferred_element_type=jnp.float32) / 8.0
    n = s.shape[0]
    row = lax.broadcasted_iota(jnp.int32, (n, n), 0)
    col = lax.broadcasted_iota(jnp.int32, (n, n), 1)
    allowed = (col <= row) & (col < len_ref[0])
    s = jnp.where(allowed, s, -1e30)
    m = jnp.max(s, axis=-1, keepdims=True)
    e = jnp.exp(s - m)
    w = (e / jnp.sum(e, axis=-1, keepdims=True)).astype(jnp.bfloat16)
    o_ref[0] = jnp.dot(w, v, preferred_element_type=jnp.float32).astype(o_ref.dtype)


def causal_attention(q, k, v, kv_of_head, length, interpret=False):
    heads, n, d = q.shape
    spec_q = pl.BlockSpec((1, n, d), lambda h, kv, ln: (h, 0, 0))
    spec_kv = pl.BlockSpec((1, n, d), lambda h, kv, ln: (kv[h], 0, 0))
    return pl.pallas_call(
        _attn_body,
        grid_spec=pltpu.PrefetchScalarGridSpec(
            num_scalar_prefetch=2,
            grid=(heads,),
            in_specs=[spec_q, spec_kv, spec_kv],
            out_specs=spec_q,
        ),
        out_shape=jax.ShapeDtypeStruct((heads, n, d), jnp.bfloat16),
        interpret=interpret,
    )(kv_of_head, length.reshape(1), q, k, v)


def pick(stack, index):
    return lax.dynamic_index_in_dim(stack, index, axis=0, keepdims=False)


def tp_reduce_scatter(partial, core_bit, chip_bit):
    rows, width = partial.shape
    halves = partial.reshape(2, rows // 2, width)
    got = lax.ppermute(pick(halves, 1 - core_bit), "tp", CHIP_PAIRS)
    first = pick(halves, core_bit).astype(jnp.float32) + got.astype(jnp.float32)
    quarters = first.reshape(2, rows // 4, width)
    sent = pick(quarters, 1 - chip_bit).astype(jnp.bfloat16)
    got = lax.ppermute(sent, "tp", CROSS_PAIRS)
    return pick(quarters, chip_bit) + got.astype(jnp.float32)


def tp_all_gather(quarter, core_bit, chip_bit):
    got = lax.ppermute(quarter, "tp", CROSS_PAIRS)
    half = jnp.zeros((2,) + quarter.shape, quarter.dtype)
    half = lax.dynamic_update_index_in_dim(half, quarter, chip_bit, 0)
    half = lax.dynamic_update_index_in_dim(half, got, 1 - chip_bit, 0)
    half = half.reshape((-1,) + quarter.shape[1:])
    got = lax.ppermute(half, "tp", CHIP_PAIRS)
    full = jnp.zeros((2,) + half.shape, half.dtype)
    full = lax.dynamic_update_index_in_dim(full, half, core_bit, 0)
    full = lax.dynamic_update_index_in_dim(full, got, 1 - core_bit, 0)
    return full.reshape((-1,) + half.shape[1:])


def ring_step(block, pos, size, shift_pairs):
    up, down = shift_pairs
    buf = jnp.zeros((size,) + block.shape, block.dtype)
    buf = lax.dynamic_update_index_in_dim(buf, block, pos, 0)
    from_below = lax.ppermute(block, "req", up)
    from_above = lax.ppermute(block, "req", down)
    buf = lax.dynamic_update_index_in_dim(buf, from_below, (pos + size - 1) % size, 0)
    buf = lax.dynamic_update_index_in_dim(buf, from_above, (pos + 1) % size, 0)
    half = block.shape[0] // 2
    far_low = lax.ppermute(from_below[:half], "req", up)
    far_high = lax.ppermute(from_above[half:], "req", down)
    far = jnp.concatenate([far_low, far_high], axis=0)
    buf = lax.dynamic_update_index_in_dim(buf, far, (pos + 2) % size, 0)
    return buf.reshape((size * block.shape[0],) + block.shape[1:])


def req_gather_stages(req_index, dims):
    nz, nx, ny = dims
    z = req_index // (nx * ny)
    x = (req_index // ny) % nx
    y = req_index % ny
    ids = [(a, b, c) for a in range(nz) for b in range(nx) for c in range(ny)]

    def lin(a, b, c):
        return (a * nx + b) * ny + c

    y_pairs = [(lin(a, b, c), lin(a, b, 1 - c)) for a, b, c in ids]
    x_pairs = (
        [(lin(a, b, c), lin(a, (b + 1) % nx, c)) for a, b, c in ids],
        [(lin(a, b, c), lin(a, (b - 1) % nx, c)) for a, b, c in ids],
    )
    z_pairs = (
        [(lin(a, b, c), lin((a + 1) % nz, b, c)) for a, b, c in ids],
        [(lin(a, b, c), lin((a - 1) % nz, b, c)) for a, b, c in ids],
    )

    def y_stage(block):
        got = lax.ppermute(block, "req", y_pairs)
        return jnp.where(
            y == 0, jnp.concatenate([block, got], 0), jnp.concatenate([got, block], 0)
        )

    def x_stage(block):
        return ring_step(block, x, nx, x_pairs)

    def z_stage(block):
        return ring_step(block, z, nz, z_pairs)

    return y_stage, x_stage, z_stage


def local(
    hidden_in,
    lengths,
    attn_gain,
    mlp_gain,
    q_master,
    k_master,
    trainer_value_weight,
    o_master,
    gate_master,
    up_master,
    down_master,
):
    tp_count = lax.axis_size("tp")
    req_count = lax.axis_size("req")
    tensor_shard_index = lax.axis_index("tp")
    core_bit = tensor_shard_index % 2
    chip_bit = tensor_shard_index // 2
    bf = jnp.bfloat16
    q_cols = q_master.shape[1] // tp_count
    kv_cols = k_master.shape[1]
    ff_cols = gate_master.shape[1] // tp_count
    local_rows = q_master.shape[0]
    model_cols = o_master.shape[1]
    block_rows = tp_count * local_rows

    def dest_chunk(dest):
        return jnp.concatenate(
            [
                q_master[:, dest * q_cols : (dest + 1) * q_cols],
                k_master,
                trainer_value_weight,
                gate_master[:, dest * ff_cols : (dest + 1) * ff_cols],
                up_master[:, dest * ff_cols : (dest + 1) * ff_cols],
            ],
            axis=1,
        ).astype(bf)

    send = jnp.stack([dest_chunk(d) for d in range(tp_count)])
    recv = lax.all_to_all(send, "tp", 0, 0, tiled=False)
    col_block = recv.reshape(block_rows, -1)
    qkv_width = q_cols + 2 * kv_cols

    o_size = o_master.size
    row_pack = jnp.concatenate([o_master.reshape(-1), down_master.reshape(-1)]).astype(bf)
    per_block = req_count // tp_count
    perm = []
    for r_src in range(req_count):
        for t_src in range(tp_count):
            r_dst = tp_count * (r_src % per_block) + t_src
            t_dst = r_src // per_block
            perm.append((r_src * tp_count + t_src, r_dst * tp_count + t_dst))
    row_pack = lax.ppermute(row_pack, ("req", "tp"), perm)

    attn_pack = jnp.concatenate(
        [col_block[:, :qkv_width], row_pack[:o_size].reshape(block_rows, -1)], axis=1
    )
    ffn_pack = jnp.concatenate(
        [col_block[:, qkv_width:], row_pack[o_size:].reshape(block_rows, -1)], axis=1
    )
    y_stage, x_stage, z_stage = req_gather_stages(lax.axis_index("req"), REQ_DIMS)
    attn_y = y_stage(attn_pack)
    ffn_y = y_stage(ffn_pack)
    attn_x = x_stage(attn_y)
    attn_x, ffn_y = lax.optimization_barrier((attn_x, ffn_y))
    ffn_x = x_stage(ffn_y)
    attn_all = z_stage(attn_x)
    attn_all, ffn_x = lax.optimization_barrier((attn_all, ffn_x))
    ffn_all = z_stage(ffn_x)
    qkv_weight = attn_all[:, :qkv_width]
    out_weight = attn_all[:, qkv_width:].reshape(req_count, -1).reshape(-1, model_cols)

    prompt_batch, sequence_length, model_width = hidden_in.shape
    local_heads = q_cols // HEAD_DIM
    cosine_table, sine_table = rope_tables(sequence_length, HEAD_DIM)
    owner_shards = (
        tensor_shard_index * local_heads + jnp.arange(local_heads, dtype=jnp.int32)
    ) // (QUERY_HEADS // KEY_VALUE_HEADS)
    quarter_rows = sequence_length // tp_count
    row_start = (core_bit * 2 + chip_bit) * quarter_rows

    def attention(prompt_rows, length):
        flat_rows = prompt_rows.astype(jnp.float32)
        normalized_input = rms_norm(flat_rows, attn_gain)
        qkv = jnp.dot(normalized_input, qkv_weight, preferred_element_type=jnp.float32)
        queries = qkv[:, :q_cols].reshape(sequence_length, local_heads, HEAD_DIM)
        key_rows = qkv[:, q_cols : q_cols + kv_cols].reshape(
            sequence_length, KEY_VALUE_HEADS, HEAD_DIM
        )
        value_rows = qkv[:, q_cols + kv_cols :].reshape(sequence_length, KEY_VALUE_HEADS, HEAD_DIM)
        q_rot = rotate(queries, cosine_table, sine_table).astype(jnp.bfloat16)
        rotated_keys = rotate(key_rows, cosine_table, sine_table).astype(jnp.bfloat16)
        value_halves = value_rows.astype(jnp.bfloat16)
        cache = jnp.concatenate(
            [
                rotated_keys.reshape(sequence_length, KEY_VALUE_HEADS * HEAD_DIM),
                value_halves.reshape(sequence_length, KEY_VALUE_HEADS * HEAD_DIM),
            ],
            axis=1,
        )
        attended = causal_attention(
            q_rot.transpose(1, 0, 2),
            rotated_keys.transpose(1, 0, 2),
            value_halves.transpose(1, 0, 2),
            owner_shards,
            length,
        )
        attended = attended.transpose(1, 0, 2).reshape(sequence_length, local_heads * HEAD_DIM)
        return flat_rows, attended, cache

    def finish(flat_rows, attended, gate_up_weight, down_weight):
        attn_partial = jnp.dot(attended, out_weight, preferred_element_type=jnp.float32).astype(bf)
        attn_mine = tp_reduce_scatter(attn_partial, core_bit, chip_bit)
        middle = lax.dynamic_slice_in_dim(flat_rows, row_start, quarter_rows, 0) + attn_mine
        normed_mine = rms_norm(middle, mlp_gain)
        normed_rows = tp_all_gather(normed_mine, core_bit, chip_bit)
        gate_up = jnp.dot(normed_rows, gate_up_weight, preferred_element_type=jnp.float32)
        gate_val = gate_up[:, :ff_cols]
        up_val = gate_up[:, ff_cols:]
        hidden_ff = (jax.nn.silu(gate_val) * up_val).astype(jnp.bfloat16)
        ffn_partial = jnp.dot(hidden_ff, down_weight, preferred_element_type=jnp.float32).astype(bf)
        ffn_mine = tp_reduce_scatter(ffn_partial, core_bit, chip_bit)
        result_mine = (middle + ffn_mine).astype(jnp.bfloat16)
        return tp_all_gather(result_mine, core_bit, chip_bit)

    firsts = [attention(hidden_in[p], lengths[p]) for p in range(prompt_batch)]
    first_attended, ffn_all = lax.optimization_barrier((firsts[0][1], ffn_all))
    gate_up_weight = ffn_all[:, : 2 * ff_cols]
    down_weight = ffn_all[:, 2 * ff_cols :].reshape(req_count, -1).reshape(-1, model_cols)
    results = []
    for p, (flat_rows, attended, _) in enumerate(firsts):
        if p == 0:
            attended = first_attended
        results.append(finish(flat_rows, attended, gate_up_weight, down_weight))
    hidden_out = jnp.stack(results)
    kv_cache = jnp.stack([cache for _, _, cache in firsts])
    return (hidden_out, kv_cache)


def solution(mesh):
    placed = (
        P("req", None, None),
        P("req"),
        P(),
        P(),
        P(("req", "tp"), None),
        P(("req", "tp"), None),
        P(("req", "tp"), None),
        P(("req", "tp"), None),
        P(("req", "tp"), None),
        P(("req", "tp"), None),
        P(("req", "tp"), None),
    )
    return jax.shard_map(
        local,
        mesh=mesh,
        in_specs=placed,
        out_specs=(P("req", None, None), P("req", None, None)),
        check_vma=False,
    )
```

```python
import math

import jax
import jax.numpy as jnp
from jax import lax
from jax.experimental import pallas as pl
from jax.experimental.pallas import tpu as pltpu
from jax.sharding import PartitionSpec as P

QUERY_HEADS = 20
KEY_VALUE_HEADS = 5
HEAD_DIM = 64


def rms_norm(field, gain_vec):
    scale = lax.rsqrt(jnp.mean(field * field, axis=-1, keepdims=True) + 1e-05)
    return (field * scale * gain_vec).astype(jnp.bfloat16)


def rope_tables(sequence_length, head_size):
    half_width = head_size // 2
    positions = jnp.arange(sequence_length, dtype=jnp.float32)[:, None]
    frequency = jnp.exp(
        -math.log(10000.0) * (2.0 * jnp.arange(half_width, dtype=jnp.float32) / head_size)
    )
    angles = positions * frequency[None, :]
    return (jnp.cos(angles), jnp.sin(angles))


def rotate(field, cosine_table, sine_table):
    half_width = field.shape[-1] // 2
    first_half = field[..., :half_width]
    second_half = field[..., half_width:]
    cos_b = cosine_table[:, None, :]
    sin_b = sine_table[:, None, :]
    return jnp.concatenate(
        [first_half * cos_b - second_half * sin_b, second_half * cos_b + first_half * sin_b],
        axis=-1,
    )


REQ_DIMS = (4, 4, 2)
CHIP_PAIRS = [(0, 1), (1, 0), (2, 3), (3, 2)]
CROSS_PAIRS = [(0, 2), (2, 0), (1, 3), (3, 1)]


def _attn_body(len_ref, q_ref, k_ref, v_ref, o_ref):
    n = q_ref.shape[0]
    row = lax.broadcasted_iota(jnp.int32, (n, n), 0)
    col = lax.broadcasted_iota(jnp.int32, (n, n), 1)
    allowed = (col <= row) & (col < len_ref[0])
    for h in range(q_ref.shape[1] // HEAD_DIM):
        cols = slice(h * HEAD_DIM, (h + 1) * HEAD_DIM)
        q = q_ref[:, cols]
        k = k_ref[:, cols]
        v = v_ref[:, cols]
        s = lax.dot_general(q, k, (((1,), (1,)), ((), ())), preferred_element_type=jnp.float32) / 8.0
        s = jnp.where(allowed, s, -1e30)
        m = jnp.max(s, axis=-1, keepdims=True)
        e = jnp.exp(s - m)
        w = (e / jnp.sum(e, axis=-1, keepdims=True)).astype(jnp.bfloat16)
        o_ref[:, cols] = jnp.dot(w, v, preferred_element_type=jnp.float32).astype(o_ref.dtype)


def causal_attention(q, k, v, length, interpret=False):
    n, width = q.shape
    full = pl.BlockSpec((n, width), lambda i, ln: (0, 0))
    return pl.pallas_call(
        _attn_body,
        grid_spec=pltpu.PrefetchScalarGridSpec(
            num_scalar_prefetch=1, grid=(1,), in_specs=[full, full, full], out_specs=full
        ),
        out_shape=jax.ShapeDtypeStruct((n, width), jnp.bfloat16),
        interpret=interpret,
    )(length.reshape(1), q, k, v)


def pick(stack, index):
    return lax.dynamic_index_in_dim(stack, index, axis=0, keepdims=False)


def tp_reduce_scatter(partial, core_bit, chip_bit):
    rows, width = partial.shape
    halves = partial.reshape(2, rows // 2, width)
    got = lax.ppermute(pick(halves, 1 - core_bit), "tp", CHIP_PAIRS)
    first = pick(halves, core_bit).astype(jnp.float32) + got.astype(jnp.float32)
    quarters = first.reshape(2, rows // 4, width)
    sent = pick(quarters, 1 - chip_bit).astype(jnp.bfloat16)
    got = lax.ppermute(sent, "tp", CROSS_PAIRS)
    return pick(quarters, chip_bit) + got.astype(jnp.float32)


def tp_all_gather(quarter, core_bit, chip_bit):
    got = lax.ppermute(quarter, "tp", CROSS_PAIRS)
    half = jnp.zeros((2,) + quarter.shape, quarter.dtype)
    half = lax.dynamic_update_index_in_dim(half, quarter, chip_bit, 0)
    half = lax.dynamic_update_index_in_dim(half, got, 1 - chip_bit, 0)
    half = half.reshape((-1,) + quarter.shape[1:])
    got = lax.ppermute(half, "tp", CHIP_PAIRS)
    full = jnp.zeros((2,) + half.shape, half.dtype)
    full = lax.dynamic_update_index_in_dim(full, half, core_bit, 0)
    full = lax.dynamic_update_index_in_dim(full, got, 1 - core_bit, 0)
    return full.reshape((-1,) + half.shape[1:])


def ring_step(block, pos, size, shift_pairs):
    up, down = shift_pairs
    buf = jnp.zeros((size,) + block.shape, block.dtype)
    buf = lax.dynamic_update_index_in_dim(buf, block, pos, 0)
    from_below = lax.ppermute(block, "req", up)
    from_above = lax.ppermute(block, "req", down)
    buf = lax.dynamic_update_index_in_dim(buf, from_below, (pos + size - 1) % size, 0)
    buf = lax.dynamic_update_index_in_dim(buf, from_above, (pos + 1) % size, 0)
    half = block.shape[0] // 2
    far_low = lax.ppermute(from_below[:half], "req", up)
    far_high = lax.ppermute(from_above[half:], "req", down)
    far = jnp.concatenate([far_low, far_high], axis=0)
    buf = lax.dynamic_update_index_in_dim(buf, far, (pos + 2) % size, 0)
    return buf.reshape((size * block.shape[0],) + block.shape[1:])


def req_gather_stages(req_index, dims):
    nz, nx, ny = dims
    z = req_index // (nx * ny)
    x = (req_index // ny) % nx
    y = req_index % ny
    ids = [(a, b, c) for a in range(nz) for b in range(nx) for c in range(ny)]

    def lin(a, b, c):
        return (a * nx + b) * ny + c

    y_pairs = [(lin(a, b, c), lin(a, b, 1 - c)) for a, b, c in ids]
    x_pairs = (
        [(lin(a, b, c), lin(a, (b + 1) % nx, c)) for a, b, c in ids],
        [(lin(a, b, c), lin(a, (b - 1) % nx, c)) for a, b, c in ids],
    )
    z_pairs = (
        [(lin(a, b, c), lin((a + 1) % nz, b, c)) for a, b, c in ids],
        [(lin(a, b, c), lin((a - 1) % nz, b, c)) for a, b, c in ids],
    )

    def y_stage(block):
        got = lax.ppermute(block, "req", y_pairs)
        return jnp.where(
            y == 0, jnp.concatenate([block, got], 0), jnp.concatenate([got, block], 0)
        )

    def x_stage(block):
        return ring_step(block, x, nx, x_pairs)

    def z_stage(block):
        return ring_step(block, z, nz, z_pairs)

    return y_stage, x_stage, z_stage


def local(
    hidden_in,
    lengths,
    attn_gain,
    mlp_gain,
    q_master,
    k_master,
    trainer_value_weight,
    o_master,
    gate_master,
    up_master,
    down_master,
):
    tp_count = lax.axis_size("tp")
    req_count = lax.axis_size("req")
    tensor_shard_index = lax.axis_index("tp")
    core_bit = tensor_shard_index % 2
    chip_bit = tensor_shard_index // 2
    bf = jnp.bfloat16
    q_cols = q_master.shape[1] // tp_count
    kv_cols = k_master.shape[1]
    ff_cols = gate_master.shape[1] // tp_count
    local_rows = q_master.shape[0]
    model_cols = o_master.shape[1]
    block_rows = tp_count * local_rows

    def dest_chunk(dest):
        return jnp.concatenate(
            [
                q_master[:, dest * q_cols : (dest + 1) * q_cols],
                k_master,
                trainer_value_weight,
                gate_master[:, dest * ff_cols : (dest + 1) * ff_cols],
                up_master[:, dest * ff_cols : (dest + 1) * ff_cols],
            ],
            axis=1,
        ).astype(bf)

    send = jnp.stack([dest_chunk(d) for d in range(tp_count)])
    recv = lax.all_to_all(send, "tp", 0, 0, tiled=False)
    col_block = recv.reshape(block_rows, -1)
    qkv_width = q_cols + 2 * kv_cols

    o_size = o_master.size
    row_pack = jnp.concatenate([o_master.reshape(-1), down_master.reshape(-1)]).astype(bf)
    per_block = req_count // tp_count
    perm = []
    for r_src in range(req_count):
        for t_src in range(tp_count):
            r_dst = tp_count * (r_src % per_block) + t_src
            t_dst = r_src // per_block
            perm.append((r_src * tp_count + t_src, r_dst * tp_count + t_dst))
    row_pack = lax.ppermute(row_pack, ("req", "tp"), perm)

    attn_pack = jnp.concatenate(
        [col_block[:, :qkv_width], row_pack[:o_size].reshape(block_rows, -1)], axis=1
    )
    ffn_pack = jnp.concatenate(
        [col_block[:, qkv_width:], row_pack[o_size:].reshape(block_rows, -1)], axis=1
    )
    y_stage, x_stage, z_stage = req_gather_stages(lax.axis_index("req"), REQ_DIMS)
    attn_y = y_stage(attn_pack)
    ffn_y = y_stage(ffn_pack)
    attn_x = x_stage(attn_y)
    attn_x, ffn_y = lax.optimization_barrier((attn_x, ffn_y))
    ffn_x = x_stage(ffn_y)
    attn_all = z_stage(attn_x)
    attn_all, ffn_x = lax.optimization_barrier((attn_all, ffn_x))
    ffn_all = z_stage(ffn_x)
    qkv_weight = attn_all[:, :qkv_width]
    out_weight = attn_all[:, qkv_width:].reshape(req_count, -1).reshape(-1, model_cols)

    prompt_batch, sequence_length, model_width = hidden_in.shape
    local_heads = q_cols // HEAD_DIM
    cosine_table, sine_table = rope_tables(sequence_length, HEAD_DIM)
    owner_shards = (
        tensor_shard_index * local_heads + jnp.arange(local_heads, dtype=jnp.int32)
    ) // (QUERY_HEADS // KEY_VALUE_HEADS)
    quarter_rows = sequence_length // tp_count
    row_start = (core_bit * 2 + chip_bit) * quarter_rows

    def attention(prompt_rows, length):
        flat_rows = prompt_rows.astype(jnp.float32)
        normalized_input = rms_norm(flat_rows, attn_gain)
        qkv = jnp.dot(normalized_input, qkv_weight, preferred_element_type=jnp.float32)
        queries = qkv[:, :q_cols].reshape(sequence_length, local_heads, HEAD_DIM)
        key_rows = qkv[:, q_cols : q_cols + kv_cols].reshape(
            sequence_length, KEY_VALUE_HEADS, HEAD_DIM
        )
        value_rows = qkv[:, q_cols + kv_cols :].reshape(sequence_length, KEY_VALUE_HEADS, HEAD_DIM)
        q_rot = rotate(queries, cosine_table, sine_table).astype(jnp.bfloat16)
        rotated_keys = rotate(key_rows, cosine_table, sine_table).astype(jnp.bfloat16)
        value_halves = value_rows.astype(jnp.bfloat16)
        cache = jnp.concatenate(
            [
                rotated_keys.reshape(sequence_length, KEY_VALUE_HEADS * HEAD_DIM),
                value_halves.reshape(sequence_length, KEY_VALUE_HEADS * HEAD_DIM),
            ],
            axis=1,
        )
        attended = causal_attention(
            q_rot.reshape(sequence_length, -1),
            jnp.take(rotated_keys, owner_shards, axis=1).reshape(sequence_length, -1),
            jnp.take(value_halves, owner_shards, axis=1).reshape(sequence_length, -1),
            length,
        )
        return flat_rows, attended, cache

    def finish(flat_rows, attended, gate_up_weight, down_weight):
        attn_partial = jnp.dot(attended, out_weight, preferred_element_type=jnp.float32).astype(bf)
        attn_mine = tp_reduce_scatter(attn_partial, core_bit, chip_bit)
        middle = lax.dynamic_slice_in_dim(flat_rows, row_start, quarter_rows, 0) + attn_mine
        normed_mine = rms_norm(middle, mlp_gain)
        normed_rows = tp_all_gather(normed_mine, core_bit, chip_bit)
        gate_up = jnp.dot(normed_rows, gate_up_weight, preferred_element_type=jnp.float32)
        gate_val = gate_up[:, :ff_cols]
        up_val = gate_up[:, ff_cols:]
        hidden_ff = (jax.nn.silu(gate_val) * up_val).astype(jnp.bfloat16)
        ffn_partial = jnp.dot(hidden_ff, down_weight, preferred_element_type=jnp.float32).astype(bf)
        ffn_mine = tp_reduce_scatter(ffn_partial, core_bit, chip_bit)
        result_mine = (middle + ffn_mine).astype(jnp.bfloat16)
        return tp_all_gather(result_mine, core_bit, chip_bit)

    firsts = [attention(hidden_in[p], lengths[p]) for p in range(prompt_batch)]
    first_attended, ffn_all = lax.optimization_barrier((firsts[0][1], ffn_all))
    gate_up_weight = ffn_all[:, : 2 * ff_cols]
    down_weight = ffn_all[:, 2 * ff_cols :].reshape(req_count, -1).reshape(-1, model_cols)
    results = []
    for p, (flat_rows, attended, _) in enumerate(firsts):
        if p == 0:
            attended = first_attended
        results.append(finish(flat_rows, attended, gate_up_weight, down_weight))
    hidden_out = jnp.stack(results)
    kv_cache = jnp.stack([cache for _, _, cache in firsts])
    return (hidden_out, kv_cache)


def solution(mesh):
    placed = (
        P("req", None, None),
        P("req"),
        P(),
        P(),
        P(("req", "tp"), None),
        P(("req", "tp"), None),
        P(("req", "tp"), None),
        P(("req", "tp"), None),
        P(("req", "tp"), None),
        P(("req", "tp"), None),
        P(("req", "tp"), None),
    )
    return jax.shard_map(
        local,
        mesh=mesh,
        in_specs=placed,
        out_specs=(P("req", None, None), P("req", None, None)),
        check_vma=False,
    )
```

```python
import math

import jax
import jax.numpy as jnp
from jax import lax
from jax.experimental import pallas as pl
from jax.experimental.pallas import tpu as pltpu
from jax.sharding import PartitionSpec as P

QUERY_HEADS = 20
KEY_VALUE_HEADS = 5
HEAD_DIM = 64


def rms_norm(field, gain_vec):
    scale = lax.rsqrt(jnp.mean(field * field, axis=-1, keepdims=True) + 1e-05)
    return (field * scale * gain_vec).astype(jnp.bfloat16)


def rope_tables(sequence_length, head_size):
    half_width = head_size // 2
    positions = jnp.arange(sequence_length, dtype=jnp.float32)[:, None]
    frequency = jnp.exp(
        -math.log(10000.0) * (2.0 * jnp.arange(half_width, dtype=jnp.float32) / head_size)
    )
    angles = positions * frequency[None, :]
    return (jnp.cos(angles), jnp.sin(angles))


def rotate(field, cosine_table, sine_table):
    half_width = field.shape[-1] // 2
    first_half = field[..., :half_width]
    second_half = field[..., half_width:]
    cos_b = cosine_table[:, None, :]
    sin_b = sine_table[:, None, :]
    return jnp.concatenate(
        [first_half * cos_b - second_half * sin_b, second_half * cos_b + first_half * sin_b],
        axis=-1,
    )


REQ_DIMS = (4, 4, 2)
CHIP_PAIRS = [(0, 1), (1, 0), (2, 3), (3, 2)]
CROSS_PAIRS = [(0, 2), (2, 0), (1, 3), (3, 1)]


def _attn_body(len_ref, q_ref, k_ref, v_ref, o_ref):
    n = q_ref.shape[0]
    row = lax.broadcasted_iota(jnp.int32, (n, n), 0)
    col = lax.broadcasted_iota(jnp.int32, (n, n), 1)
    allowed = (col <= row) & (col < len_ref[0])
    for h in range(q_ref.shape[1] // HEAD_DIM):
        cols = slice(h * HEAD_DIM, (h + 1) * HEAD_DIM)
        q = q_ref[:, cols]
        k = k_ref[:, cols]
        v = v_ref[:, cols]
        s = lax.dot_general(q, k, (((1,), (1,)), ((), ())), preferred_element_type=jnp.float32) / 8.0
        s = jnp.where(allowed, s, -1e30)
        m = jnp.max(s, axis=-1, keepdims=True)
        e = jnp.exp(s - m)
        w = (e / jnp.sum(e, axis=-1, keepdims=True)).astype(jnp.bfloat16)
        o_ref[:, cols] = jnp.dot(w, v, preferred_element_type=jnp.float32).astype(o_ref.dtype)


def causal_attention(q, k, v, length, interpret=False):
    n, width = q.shape
    full = pl.BlockSpec((n, width), lambda i, ln: (0, 0))
    return pl.pallas_call(
        _attn_body,
        grid_spec=pltpu.PrefetchScalarGridSpec(
            num_scalar_prefetch=1, grid=(1,), in_specs=[full, full, full], out_specs=full
        ),
        out_shape=jax.ShapeDtypeStruct((n, width), jnp.bfloat16),
        interpret=interpret,
    )(length.reshape(1), q, k, v)


def pick(stack, index):
    return lax.dynamic_index_in_dim(stack, index, axis=0, keepdims=False)


def tp_reduce_scatter(partial, core_bit, chip_bit):
    rows, width = partial.shape
    halves = partial.reshape(2, rows // 2, width)
    got = lax.ppermute(pick(halves, 1 - core_bit), "tp", CHIP_PAIRS)
    first = pick(halves, core_bit).astype(jnp.float32) + got.astype(jnp.float32)
    quarters = first.reshape(2, rows // 4, width)
    sent = pick(quarters, 1 - chip_bit).astype(jnp.bfloat16)
    got = lax.ppermute(sent, "tp", CROSS_PAIRS)
    return pick(quarters, chip_bit) + got.astype(jnp.float32)


def tp_all_gather(quarter, core_bit, chip_bit):
    got = lax.ppermute(quarter, "tp", CROSS_PAIRS)
    half = jnp.zeros((2,) + quarter.shape, quarter.dtype)
    half = lax.dynamic_update_index_in_dim(half, quarter, chip_bit, 0)
    half = lax.dynamic_update_index_in_dim(half, got, 1 - chip_bit, 0)
    half = half.reshape((-1,) + quarter.shape[1:])
    got = lax.ppermute(half, "tp", CHIP_PAIRS)
    full = jnp.zeros((2,) + half.shape, half.dtype)
    full = lax.dynamic_update_index_in_dim(full, half, core_bit, 0)
    full = lax.dynamic_update_index_in_dim(full, got, 1 - core_bit, 0)
    return full.reshape((-1,) + half.shape[1:])


def ring_step(block, pos, size, shift_pairs):
    up, down = shift_pairs
    buf = jnp.zeros((size,) + block.shape, block.dtype)
    buf = lax.dynamic_update_index_in_dim(buf, block, pos, 0)
    from_below = lax.ppermute(block, "req", up)
    from_above = lax.ppermute(block, "req", down)
    buf = lax.dynamic_update_index_in_dim(buf, from_below, (pos + size - 1) % size, 0)
    buf = lax.dynamic_update_index_in_dim(buf, from_above, (pos + 1) % size, 0)
    half = block.shape[0] // 2
    far_low = lax.ppermute(from_below[:half], "req", up)
    far_high = lax.ppermute(from_above[half:], "req", down)
    far = jnp.concatenate([far_low, far_high], axis=0)
    buf = lax.dynamic_update_index_in_dim(buf, far, (pos + 2) % size, 0)
    return buf.reshape((size * block.shape[0],) + block.shape[1:])


def req_gather_stages(req_index, dims):
    nz, nx, ny = dims
    z = req_index // (nx * ny)
    x = (req_index // ny) % nx
    y = req_index % ny
    ids = [(a, b, c) for a in range(nz) for b in range(nx) for c in range(ny)]

    def lin(a, b, c):
        return (a * nx + b) * ny + c

    y_pairs = [(lin(a, b, c), lin(a, b, 1 - c)) for a, b, c in ids]
    x_pairs = (
        [(lin(a, b, c), lin(a, (b + 1) % nx, c)) for a, b, c in ids],
        [(lin(a, b, c), lin(a, (b - 1) % nx, c)) for a, b, c in ids],
    )
    z_pairs = (
        [(lin(a, b, c), lin((a + 1) % nz, b, c)) for a, b, c in ids],
        [(lin(a, b, c), lin((a - 1) % nz, b, c)) for a, b, c in ids],
    )

    def y_stage(block):
        got = lax.ppermute(block, "req", y_pairs)
        return jnp.where(
            y == 0, jnp.concatenate([block, got], 0), jnp.concatenate([got, block], 0)
        )

    def x_stage(block):
        return ring_step(block, x, nx, x_pairs)

    def z_stage(block):
        return ring_step(block, z, nz, z_pairs)

    return y_stage, x_stage, z_stage


def local(
    hidden_in,
    lengths,
    attn_gain,
    mlp_gain,
    q_master,
    k_master,
    trainer_value_weight,
    o_master,
    gate_master,
    up_master,
    down_master,
):
    tp_count = lax.axis_size("tp")
    req_count = lax.axis_size("req")
    tensor_shard_index = lax.axis_index("tp")
    core_bit = tensor_shard_index % 2
    chip_bit = tensor_shard_index // 2
    bf = jnp.bfloat16
    q_cols = q_master.shape[1] // tp_count
    kv_cols = k_master.shape[1]
    ff_cols = gate_master.shape[1] // tp_count
    local_rows = q_master.shape[0]
    model_cols = o_master.shape[1]
    block_rows = tp_count * local_rows

    def dest_chunk(dest):
        return jnp.concatenate(
            [
                q_master[:, dest * q_cols : (dest + 1) * q_cols],
                k_master,
                trainer_value_weight,
                gate_master[:, dest * ff_cols : (dest + 1) * ff_cols],
                up_master[:, dest * ff_cols : (dest + 1) * ff_cols],
            ],
            axis=1,
        ).astype(bf)

    send = jnp.stack([dest_chunk(d) for d in range(tp_count)])
    recv = lax.all_to_all(send, "tp", 0, 0, tiled=False)
    col_block = recv.reshape(block_rows, -1)
    qkv_width = q_cols + 2 * kv_cols

    o_size = o_master.size
    row_pack = jnp.concatenate([o_master.reshape(-1), down_master.reshape(-1)]).astype(bf)
    per_block = req_count // tp_count
    perm = []
    for r_src in range(req_count):
        for t_src in range(tp_count):
            r_dst = tp_count * (r_src % per_block) + t_src
            t_dst = r_src // per_block
            perm.append((r_src * tp_count + t_src, r_dst * tp_count + t_dst))
    row_pack = lax.ppermute(row_pack, ("req", "tp"), perm)

    attn_pack = jnp.concatenate(
        [col_block[:, :qkv_width], row_pack[:o_size].reshape(block_rows, -1)], axis=1
    )
    ffn_pack = jnp.concatenate(
        [col_block[:, qkv_width:], row_pack[o_size:].reshape(block_rows, -1)], axis=1
    )
    y_stage, x_stage, z_stage = req_gather_stages(lax.axis_index("req"), REQ_DIMS)
    attn_y = y_stage(attn_pack)
    ffn_y = y_stage(ffn_pack)
    attn_x = x_stage(attn_y)
    ffn_z = z_stage(ffn_y)
    attn_x, ffn_z = lax.optimization_barrier((attn_x, ffn_z))
    attn_all = z_stage(attn_x)
    ffn_xz = x_stage(ffn_z)
    nz, nx, _ = REQ_DIMS
    ffn_all = (
        ffn_xz.reshape((nx, nz, -1) + ffn_xz.shape[1:])
        .transpose(1, 0, 2, 3)
        .reshape(ffn_xz.shape)
    )
    qkv_weight = attn_all[:, :qkv_width]
    out_weight = attn_all[:, qkv_width:].reshape(req_count, -1).reshape(-1, model_cols)

    prompt_batch, sequence_length, model_width = hidden_in.shape
    local_heads = q_cols // HEAD_DIM
    cosine_table, sine_table = rope_tables(sequence_length, HEAD_DIM)
    owner_shards = (
        tensor_shard_index * local_heads + jnp.arange(local_heads, dtype=jnp.int32)
    ) // (QUERY_HEADS // KEY_VALUE_HEADS)
    quarter_rows = sequence_length // tp_count
    row_start = (core_bit * 2 + chip_bit) * quarter_rows

    def attention(prompt_rows, length):
        flat_rows = prompt_rows.astype(jnp.float32)
        normalized_input = rms_norm(flat_rows, attn_gain)
        qkv = jnp.dot(normalized_input, qkv_weight, preferred_element_type=jnp.float32)
        queries = qkv[:, :q_cols].reshape(sequence_length, local_heads, HEAD_DIM)
        key_rows = qkv[:, q_cols : q_cols + kv_cols].reshape(
            sequence_length, KEY_VALUE_HEADS, HEAD_DIM
        )
        value_rows = qkv[:, q_cols + kv_cols :].reshape(sequence_length, KEY_VALUE_HEADS, HEAD_DIM)
        q_rot = rotate(queries, cosine_table, sine_table).astype(jnp.bfloat16)
        rotated_keys = rotate(key_rows, cosine_table, sine_table).astype(jnp.bfloat16)
        value_halves = value_rows.astype(jnp.bfloat16)
        cache = jnp.concatenate(
            [
                rotated_keys.reshape(sequence_length, KEY_VALUE_HEADS * HEAD_DIM),
                value_halves.reshape(sequence_length, KEY_VALUE_HEADS * HEAD_DIM),
            ],
            axis=1,
        )
        attended = causal_attention(
            q_rot.reshape(sequence_length, -1),
            jnp.take(rotated_keys, owner_shards, axis=1).reshape(sequence_length, -1),
            jnp.take(value_halves, owner_shards, axis=1).reshape(sequence_length, -1),
            length,
        )
        return flat_rows, attended, cache

    def finish(flat_rows, attended, gate_up_weight, down_weight):
        attn_partial = jnp.dot(attended, out_weight, preferred_element_type=jnp.float32).astype(bf)
        attn_mine = tp_reduce_scatter(attn_partial, core_bit, chip_bit)
        middle = lax.dynamic_slice_in_dim(flat_rows, row_start, quarter_rows, 0) + attn_mine
        normed_mine = rms_norm(middle, mlp_gain)
        normed_rows = tp_all_gather(normed_mine, core_bit, chip_bit)
        gate_up = jnp.dot(normed_rows, gate_up_weight, preferred_element_type=jnp.float32)
        gate_val = gate_up[:, :ff_cols]
        up_val = gate_up[:, ff_cols:]
        hidden_ff = (jax.nn.silu(gate_val) * up_val).astype(jnp.bfloat16)
        ffn_partial = jnp.dot(hidden_ff, down_weight, preferred_element_type=jnp.float32).astype(bf)
        ffn_mine = tp_reduce_scatter(ffn_partial, core_bit, chip_bit)
        result_mine = (middle + ffn_mine).astype(jnp.bfloat16)
        return tp_all_gather(result_mine, core_bit, chip_bit)

    firsts = [attention(hidden_in[p], lengths[p]) for p in range(prompt_batch)]
    first_attended, ffn_all = lax.optimization_barrier((firsts[0][1], ffn_all))
    gate_up_weight = ffn_all[:, : 2 * ff_cols]
    down_weight = ffn_all[:, 2 * ff_cols :].reshape(req_count, -1).reshape(-1, model_cols)
    results = []
    for p, (flat_rows, attended, _) in enumerate(firsts):
        if p == 0:
            attended = first_attended
        results.append(finish(flat_rows, attended, gate_up_weight, down_weight))
    hidden_out = jnp.stack(results)
    kv_cache = jnp.stack([cache for _, _, cache in firsts])
    return (hidden_out, kv_cache)


def solution(mesh):
    placed = (
        P("req", None, None),
        P("req"),
        P(),
        P(),
        P(("req", "tp"), None),
        P(("req", "tp"), None),
        P(("req", "tp"), None),
        P(("req", "tp"), None),
        P(("req", "tp"), None),
        P(("req", "tp"), None),
        P(("req", "tp"), None),
    )
    return jax.shard_map(
        local,
        mesh=mesh,
        in_specs=placed,
        out_specs=(P("req", None, None), P("req", None, None)),
        check_vma=False,
    )
```

```python
import math

import jax
import jax.numpy as jnp
from jax import lax
from jax.experimental import pallas as pl
from jax.experimental.pallas import tpu as pltpu
from jax.sharding import PartitionSpec as P

QUERY_HEADS = 20
KEY_VALUE_HEADS = 5
HEAD_DIM = 64


def rms_norm(field, gain_vec):
    scale = lax.rsqrt(jnp.mean(field * field, axis=-1, keepdims=True) + 1e-05)
    return (field * scale * gain_vec).astype(jnp.bfloat16)


def rope_tables(sequence_length, head_size):
    half_width = head_size // 2
    positions = jnp.arange(sequence_length, dtype=jnp.float32)[:, None]
    frequency = jnp.exp(
        -math.log(10000.0) * (2.0 * jnp.arange(half_width, dtype=jnp.float32) / head_size)
    )
    angles = positions * frequency[None, :]
    return (jnp.cos(angles), jnp.sin(angles))


def rotate(field, cosine_table, sine_table):
    half_width = field.shape[-1] // 2
    first_half = field[..., :half_width]
    second_half = field[..., half_width:]
    cos_b = cosine_table[:, None, :]
    sin_b = sine_table[:, None, :]
    return jnp.concatenate(
        [first_half * cos_b - second_half * sin_b, second_half * cos_b + first_half * sin_b],
        axis=-1,
    )


REQ_DIMS = (4, 4, 2)
CHIP_PAIRS = [(0, 1), (1, 0), (2, 3), (3, 2)]
CROSS_PAIRS = [(0, 2), (2, 0), (1, 3), (3, 1)]


def _attn_body(len_ref, q_ref, k_ref, v_ref, o_ref):
    n = q_ref.shape[0]
    row = lax.broadcasted_iota(jnp.int32, (n, n), 0)
    col = lax.broadcasted_iota(jnp.int32, (n, n), 1)
    allowed = (col <= row) & (col < len_ref[0])
    for h in range(q_ref.shape[1] // HEAD_DIM):
        cols = slice(h * HEAD_DIM, (h + 1) * HEAD_DIM)
        q = q_ref[:, cols]
        k = k_ref[:, cols]
        v = v_ref[:, cols]
        s = lax.dot_general(q, k, (((1,), (1,)), ((), ())), preferred_element_type=jnp.float32) / 8.0
        s = jnp.where(allowed, s, -1e30)
        m = jnp.max(s, axis=-1, keepdims=True)
        e = jnp.exp(s - m)
        w = (e / jnp.sum(e, axis=-1, keepdims=True)).astype(jnp.bfloat16)
        o_ref[:, cols] = jnp.dot(w, v, preferred_element_type=jnp.float32).astype(o_ref.dtype)


def causal_attention(q, k, v, length, interpret=False):
    n, width = q.shape
    full = pl.BlockSpec((n, width), lambda i, ln: (0, 0))
    return pl.pallas_call(
        _attn_body,
        grid_spec=pltpu.PrefetchScalarGridSpec(
            num_scalar_prefetch=1, grid=(1,), in_specs=[full, full, full], out_specs=full
        ),
        out_shape=jax.ShapeDtypeStruct((n, width), jnp.bfloat16),
        interpret=interpret,
    )(length.reshape(1), q, k, v)


def pick(stack, index):
    return lax.dynamic_index_in_dim(stack, index, axis=0, keepdims=False)


def tp_reduce_scatter(partial, core_bit, chip_bit):
    rows, width = partial.shape
    halves = partial.reshape(2, rows // 2, width)
    got = lax.ppermute(pick(halves, 1 - core_bit), "tp", CHIP_PAIRS)
    first = pick(halves, core_bit).astype(jnp.float32) + got.astype(jnp.float32)
    quarters = first.reshape(2, rows // 4, width)
    sent = pick(quarters, 1 - chip_bit).astype(jnp.bfloat16)
    got = lax.ppermute(sent, "tp", CROSS_PAIRS)
    return pick(quarters, chip_bit) + got.astype(jnp.float32)


def tp_all_gather(quarter, core_bit, chip_bit):
    got = lax.ppermute(quarter, "tp", CROSS_PAIRS)
    half = jnp.zeros((2,) + quarter.shape, quarter.dtype)
    half = lax.dynamic_update_index_in_dim(half, quarter, chip_bit, 0)
    half = lax.dynamic_update_index_in_dim(half, got, 1 - chip_bit, 0)
    half = half.reshape((-1,) + quarter.shape[1:])
    got = lax.ppermute(half, "tp", CHIP_PAIRS)
    full = jnp.zeros((2,) + half.shape, half.dtype)
    full = lax.dynamic_update_index_in_dim(full, half, core_bit, 0)
    full = lax.dynamic_update_index_in_dim(full, got, 1 - core_bit, 0)
    return full.reshape((-1,) + half.shape[1:])


def ring_step(block, pos, size, shift_pairs):
    up, down = shift_pairs
    buf = jnp.zeros((size,) + block.shape, block.dtype)
    buf = lax.dynamic_update_index_in_dim(buf, block, pos, 0)
    from_below = lax.ppermute(block, "req", up)
    from_above = lax.ppermute(block, "req", down)
    buf = lax.dynamic_update_index_in_dim(buf, from_below, (pos + size - 1) % size, 0)
    buf = lax.dynamic_update_index_in_dim(buf, from_above, (pos + 1) % size, 0)
    half = block.shape[0] // 2
    far_low = lax.ppermute(from_below[:half], "req", up)
    far_high = lax.ppermute(from_above[half:], "req", down)
    far = jnp.concatenate([far_low, far_high], axis=0)
    buf = lax.dynamic_update_index_in_dim(buf, far, (pos + 2) % size, 0)
    return buf.reshape((size * block.shape[0],) + block.shape[1:])


def req_gather_stages(req_index, dims):
    nz, nx, ny = dims
    z = req_index // (nx * ny)
    x = (req_index // ny) % nx
    y = req_index % ny
    ids = [(a, b, c) for a in range(nz) for b in range(nx) for c in range(ny)]

    def lin(a, b, c):
        return (a * nx + b) * ny + c

    y_pairs = [(lin(a, b, c), lin(a, b, 1 - c)) for a, b, c in ids]
    x_pairs = (
        [(lin(a, b, c), lin(a, (b + 1) % nx, c)) for a, b, c in ids],
        [(lin(a, b, c), lin(a, (b - 1) % nx, c)) for a, b, c in ids],
    )
    z_pairs = (
        [(lin(a, b, c), lin((a + 1) % nz, b, c)) for a, b, c in ids],
        [(lin(a, b, c), lin((a - 1) % nz, b, c)) for a, b, c in ids],
    )

    def y_stage(block):
        got = lax.ppermute(block, "req", y_pairs)
        return jnp.where(
            y == 0, jnp.concatenate([block, got], 0), jnp.concatenate([got, block], 0)
        )

    def x_stage(block):
        return ring_step(block, x, nx, x_pairs)

    def z_stage(block):
        return ring_step(block, z, nz, z_pairs)

    return y_stage, x_stage, z_stage


def local(
    hidden_in,
    lengths,
    attn_gain,
    mlp_gain,
    q_master,
    k_master,
    trainer_value_weight,
    o_master,
    gate_master,
    up_master,
    down_master,
):
    tp_count = lax.axis_size("tp")
    req_count = lax.axis_size("req")
    tensor_shard_index = lax.axis_index("tp")
    core_bit = tensor_shard_index % 2
    chip_bit = tensor_shard_index // 2
    bf = jnp.bfloat16
    q_cols = q_master.shape[1] // tp_count
    kv_cols = k_master.shape[1]
    ff_cols = gate_master.shape[1] // tp_count
    local_rows = q_master.shape[0]
    model_cols = o_master.shape[1]
    block_rows = tp_count * local_rows

    def dest_chunk(dest):
        return jnp.concatenate(
            [
                q_master[:, dest * q_cols : (dest + 1) * q_cols],
                k_master,
                trainer_value_weight,
                gate_master[:, dest * ff_cols : (dest + 1) * ff_cols],
                up_master[:, dest * ff_cols : (dest + 1) * ff_cols],
            ],
            axis=1,
        ).astype(bf)

    send = jnp.stack([dest_chunk(d) for d in range(tp_count)])
    recv = lax.all_to_all(send, "tp", 0, 0, tiled=False)
    col_block = recv.reshape(block_rows, -1)
    qkv_width = q_cols + 2 * kv_cols

    o_size = o_master.size
    row_pack = jnp.concatenate([o_master.reshape(-1), down_master.reshape(-1)]).astype(bf)
    per_block = req_count // tp_count
    perm = []
    for r_src in range(req_count):
        for t_src in range(tp_count):
            r_dst = tp_count * (r_src % per_block) + t_src
            t_dst = r_src // per_block
            perm.append((r_src * tp_count + t_src, r_dst * tp_count + t_dst))
    row_pack = lax.ppermute(row_pack, ("req", "tp"), perm)

    attn_pack = jnp.concatenate(
        [col_block[:, :qkv_width], row_pack[:o_size].reshape(block_rows, -1)], axis=1
    )
    ffn_pack = jnp.concatenate(
        [col_block[:, qkv_width:], row_pack[o_size:].reshape(block_rows, -1)], axis=1
    )
    y_stage, x_stage, z_stage = req_gather_stages(lax.axis_index("req"), REQ_DIMS)
    attn_y = y_stage(attn_pack)
    ffn_y = y_stage(ffn_pack)
    attn_x = x_stage(attn_y)
    ffn_z = z_stage(ffn_y)
    attn_x, ffn_z = lax.optimization_barrier((attn_x, ffn_z))
    attn_all = z_stage(attn_x)
    ffn_xz = x_stage(ffn_z)
    nz, nx, _ = REQ_DIMS
    ffn_all = (
        ffn_xz.reshape((nx, nz, -1) + ffn_xz.shape[1:])
        .transpose(1, 0, 2, 3)
        .reshape(ffn_xz.shape)
    )
    qkv_weight = attn_all[:, :qkv_width]
    out_weight = attn_all[:, qkv_width:].reshape(req_count, -1).reshape(-1, model_cols)

    prompt_batch, sequence_length, model_width = hidden_in.shape
    local_heads = q_cols // HEAD_DIM
    cosine_table, sine_table = rope_tables(sequence_length, HEAD_DIM)
    owner_shards = (
        tensor_shard_index * local_heads + jnp.arange(local_heads, dtype=jnp.int32)
    ) // (QUERY_HEADS // KEY_VALUE_HEADS)
    half = HEAD_DIM // 2
    lane = jnp.arange(q_cols) % HEAD_DIM
    first = (lane < half)[None, :]
    cos_cols = cosine_table[:, lane % half]
    sin_cols = jnp.where(first, -sine_table[:, lane % half], sine_table[:, lane % half])

    def rotate_flat(field):
        partner = jnp.where(first, jnp.roll(field, -half, axis=1), jnp.roll(field, half, axis=1))
        return field * cos_cols + partner * sin_cols

    kv_col = jnp.arange(kv_cols)
    q_col = jnp.arange(q_cols)
    head_select = (
        (kv_col[:, None] // HEAD_DIM == owner_shards[q_col // HEAD_DIM][None, :])
        & (kv_col[:, None] % HEAD_DIM == q_col[None, :] % HEAD_DIM)
    ).astype(jnp.bfloat16)
    quarter_rows = sequence_length // tp_count
    row_start = (core_bit * 2 + chip_bit) * quarter_rows

    def attention(prompt_rows, length):
        flat_rows = prompt_rows.astype(jnp.float32)
        normalized_input = rms_norm(flat_rows, attn_gain)
        qkv = jnp.dot(normalized_input, qkv_weight, preferred_element_type=jnp.float32)
        q_rot = rotate_flat(qkv[:, :q_cols]).astype(jnp.bfloat16)
        rotated_keys = rotate_flat(qkv[:, q_cols : q_cols + kv_cols]).astype(jnp.bfloat16)
        value_halves = qkv[:, q_cols + kv_cols :].astype(jnp.bfloat16)
        cache = jnp.concatenate([rotated_keys, value_halves], axis=1)
        attended = causal_attention(
            q_rot,
            jnp.dot(rotated_keys, head_select, preferred_element_type=jnp.float32).astype(bf),
            jnp.dot(value_halves, head_select, preferred_element_type=jnp.float32).astype(bf),
            length,
        )
        return flat_rows, attended, cache

    def finish(flat_rows, attended, gate_up_weight, down_weight):
        attn_partial = jnp.dot(attended, out_weight, preferred_element_type=jnp.float32).astype(bf)
        attn_mine = tp_reduce_scatter(attn_partial, core_bit, chip_bit)
        middle = lax.dynamic_slice_in_dim(flat_rows, row_start, quarter_rows, 0) + attn_mine
        normed_mine = rms_norm(middle, mlp_gain)
        normed_rows = tp_all_gather(normed_mine, core_bit, chip_bit)
        gate_up = jnp.dot(normed_rows, gate_up_weight, preferred_element_type=jnp.float32)
        gate_val = gate_up[:, :ff_cols]
        up_val = gate_up[:, ff_cols:]
        hidden_ff = (jax.nn.silu(gate_val) * up_val).astype(jnp.bfloat16)
        ffn_partial = jnp.dot(hidden_ff, down_weight, preferred_element_type=jnp.float32).astype(bf)
        ffn_mine = tp_reduce_scatter(ffn_partial, core_bit, chip_bit)
        result_mine = (middle + ffn_mine).astype(jnp.bfloat16)
        return tp_all_gather(result_mine, core_bit, chip_bit)

    firsts = [attention(hidden_in[p], lengths[p]) for p in range(prompt_batch)]
    first_attended, ffn_all = lax.optimization_barrier((firsts[0][1], ffn_all))
    gate_up_weight = ffn_all[:, : 2 * ff_cols]
    down_weight = ffn_all[:, 2 * ff_cols :].reshape(req_count, -1).reshape(-1, model_cols)
    results = []
    for p, (flat_rows, attended, _) in enumerate(firsts):
        if p == 0:
            attended = first_attended
        results.append(finish(flat_rows, attended, gate_up_weight, down_weight))
    hidden_out = jnp.stack(results)
    kv_cache = jnp.stack([cache for _, _, cache in firsts])
    return (hidden_out, kv_cache)


def solution(mesh):
    placed = (
        P("req", None, None),
        P("req"),
        P(),
        P(),
        P(("req", "tp"), None),
        P(("req", "tp"), None),
        P(("req", "tp"), None),
        P(("req", "tp"), None),
        P(("req", "tp"), None),
        P(("req", "tp"), None),
        P(("req", "tp"), None),
    )
    return jax.shard_map(
        local,
        mesh=mesh,
        in_specs=placed,
        out_specs=(P("req", None, None), P("req", None, None)),
        check_vma=False,
    )
```

```python
import math

import jax
import jax.numpy as jnp
from jax import lax
from jax.experimental import pallas as pl
from jax.experimental.pallas import tpu as pltpu
from jax.sharding import PartitionSpec as P

QUERY_HEADS = 20
KEY_VALUE_HEADS = 5
HEAD_DIM = 64


def rms_norm(field, gain_vec):
    scale = lax.rsqrt(jnp.mean(field * field, axis=-1, keepdims=True) + 1e-05)
    return (field * scale * gain_vec).astype(jnp.bfloat16)


def rope_tables(sequence_length, head_size):
    half_width = head_size // 2
    positions = jnp.arange(sequence_length, dtype=jnp.float32)[:, None]
    frequency = jnp.exp(
        -math.log(10000.0) * (2.0 * jnp.arange(half_width, dtype=jnp.float32) / head_size)
    )
    angles = positions * frequency[None, :]
    return (jnp.cos(angles), jnp.sin(angles))


def rotate(field, cosine_table, sine_table):
    half_width = field.shape[-1] // 2
    first_half = field[..., :half_width]
    second_half = field[..., half_width:]
    cos_b = cosine_table[:, None, :]
    sin_b = sine_table[:, None, :]
    return jnp.concatenate(
        [first_half * cos_b - second_half * sin_b, second_half * cos_b + first_half * sin_b],
        axis=-1,
    )


REQ_DIMS = (4, 4, 2)
CHIP_PAIRS = [(0, 1), (1, 0), (2, 3), (3, 2)]
CROSS_PAIRS = [(0, 2), (2, 0), (1, 3), (3, 1)]


def _attn_body(len_ref, q_ref, k_ref, v_ref, o_ref):
    n = q_ref.shape[0]
    row = lax.broadcasted_iota(jnp.int32, (n, n), 0)
    col = lax.broadcasted_iota(jnp.int32, (n, n), 1)
    allowed = (col <= row) & (col < len_ref[0])
    for h in range(q_ref.shape[1] // HEAD_DIM):
        cols = slice(h * HEAD_DIM, (h + 1) * HEAD_DIM)
        q = q_ref[:, cols]
        k = k_ref[:, cols]
        v = v_ref[:, cols]
        s = lax.dot_general(q, k, (((1,), (1,)), ((), ())), preferred_element_type=jnp.float32) / 8.0
        s = jnp.where(allowed, s, -1e30)
        m = jnp.max(s, axis=-1, keepdims=True)
        e = jnp.exp(s - m)
        w = (e / jnp.sum(e, axis=-1, keepdims=True)).astype(jnp.bfloat16)
        o_ref[:, cols] = jnp.dot(w, v, preferred_element_type=jnp.float32).astype(o_ref.dtype)


def causal_attention(q, k, v, length, interpret=False):
    n, width = q.shape
    full = pl.BlockSpec((n, width), lambda i, ln: (0, 0))
    return pl.pallas_call(
        _attn_body,
        grid_spec=pltpu.PrefetchScalarGridSpec(
            num_scalar_prefetch=1, grid=(1,), in_specs=[full, full, full], out_specs=full
        ),
        out_shape=jax.ShapeDtypeStruct((n, width), jnp.bfloat16),
        interpret=interpret,
    )(length.reshape(1), q, k, v)


def pick(stack, index):
    return lax.dynamic_index_in_dim(stack, index, axis=0, keepdims=False)


def tp_reduce_scatter(partial, core_bit, chip_bit):
    rows, width = partial.shape
    halves = partial.reshape(2, rows // 2, width)
    got = lax.ppermute(pick(halves, 1 - core_bit), "tp", CHIP_PAIRS)
    first = pick(halves, core_bit).astype(jnp.float32) + got.astype(jnp.float32)
    quarters = first.reshape(2, rows // 4, width)
    sent = pick(quarters, 1 - chip_bit).astype(jnp.bfloat16)
    got = lax.ppermute(sent, "tp", CROSS_PAIRS)
    return pick(quarters, chip_bit) + got.astype(jnp.float32)


def tp_all_gather(quarter, core_bit, chip_bit):
    got = lax.ppermute(quarter, "tp", CROSS_PAIRS)
    half = jnp.zeros((2,) + quarter.shape, quarter.dtype)
    half = lax.dynamic_update_index_in_dim(half, quarter, chip_bit, 0)
    half = lax.dynamic_update_index_in_dim(half, got, 1 - chip_bit, 0)
    half = half.reshape((-1,) + quarter.shape[1:])
    got = lax.ppermute(half, "tp", CHIP_PAIRS)
    full = jnp.zeros((2,) + half.shape, half.dtype)
    full = lax.dynamic_update_index_in_dim(full, half, core_bit, 0)
    full = lax.dynamic_update_index_in_dim(full, got, 1 - core_bit, 0)
    return full.reshape((-1,) + half.shape[1:])


def ring_step(block, pos, size, shift_pairs):
    up, down = shift_pairs
    buf = jnp.zeros((size,) + block.shape, block.dtype)
    buf = lax.dynamic_update_index_in_dim(buf, block, pos, 0)
    from_below = lax.ppermute(block, "req", up)
    from_above = lax.ppermute(block, "req", down)
    buf = lax.dynamic_update_index_in_dim(buf, from_below, (pos + size - 1) % size, 0)
    buf = lax.dynamic_update_index_in_dim(buf, from_above, (pos + 1) % size, 0)
    half = block.shape[0] // 2
    far_low = lax.ppermute(from_below[:half], "req", up)
    far_high = lax.ppermute(from_above[half:], "req", down)
    far = jnp.concatenate([far_low, far_high], axis=0)
    buf = lax.dynamic_update_index_in_dim(buf, far, (pos + 2) % size, 0)
    return buf.reshape((size * block.shape[0],) + block.shape[1:])


def req_gather_stages(req_index, dims):
    nz, nx, ny = dims
    z = req_index // (nx * ny)
    x = (req_index // ny) % nx
    y = req_index % ny
    ids = [(a, b, c) for a in range(nz) for b in range(nx) for c in range(ny)]

    def lin(a, b, c):
        return (a * nx + b) * ny + c

    y_pairs = [(lin(a, b, c), lin(a, b, 1 - c)) for a, b, c in ids]
    x_pairs = (
        [(lin(a, b, c), lin(a, (b + 1) % nx, c)) for a, b, c in ids],
        [(lin(a, b, c), lin(a, (b - 1) % nx, c)) for a, b, c in ids],
    )
    z_pairs = (
        [(lin(a, b, c), lin((a + 1) % nz, b, c)) for a, b, c in ids],
        [(lin(a, b, c), lin((a - 1) % nz, b, c)) for a, b, c in ids],
    )

    def y_stage(block):
        got = lax.ppermute(block, "req", y_pairs)
        return jnp.where(
            y == 0, jnp.concatenate([block, got], 0), jnp.concatenate([got, block], 0)
        )

    def x_stage(block):
        return ring_step(block, x, nx, x_pairs)

    def z_stage(block):
        return ring_step(block, z, nz, z_pairs)

    return y_stage, x_stage, z_stage


def local(
    hidden_in,
    lengths,
    attn_gain,
    mlp_gain,
    q_master,
    k_master,
    trainer_value_weight,
    o_master,
    gate_master,
    up_master,
    down_master,
):
    tp_count = lax.axis_size("tp")
    req_count = lax.axis_size("req")
    tensor_shard_index = lax.axis_index("tp")
    core_bit = tensor_shard_index % 2
    chip_bit = tensor_shard_index // 2
    bf = jnp.bfloat16
    q_cols = q_master.shape[1] // tp_count
    kv_cols = k_master.shape[1]
    ff_cols = gate_master.shape[1] // tp_count
    local_rows = q_master.shape[0]
    model_cols = o_master.shape[1]
    block_rows = tp_count * local_rows

    def dest_chunk(dest):
        return jnp.concatenate(
            [
                q_master[:, dest * q_cols : (dest + 1) * q_cols],
                k_master,
                trainer_value_weight,
                gate_master[:, dest * ff_cols : (dest + 1) * ff_cols],
                up_master[:, dest * ff_cols : (dest + 1) * ff_cols],
            ],
            axis=1,
        ).astype(bf)

    send = jnp.stack([dest_chunk(d) for d in range(tp_count)])
    recv = lax.all_to_all(send, "tp", 0, 0, tiled=False)
    col_block = recv.reshape(block_rows, -1)
    qkv_width = q_cols + 2 * kv_cols

    o_size = o_master.size
    row_pack = jnp.concatenate([o_master.reshape(-1), down_master.reshape(-1)]).astype(bf)
    per_block = req_count // tp_count
    perm = []
    for r_src in range(req_count):
        for t_src in range(tp_count):
            r_dst = tp_count * (r_src % per_block) + t_src
            t_dst = r_src // per_block
            perm.append((r_src * tp_count + t_src, r_dst * tp_count + t_dst))
    row_pack = lax.ppermute(row_pack, ("req", "tp"), perm)

    attn_pack = jnp.concatenate(
        [col_block[:, :qkv_width], row_pack[:o_size].reshape(block_rows, -1)], axis=1
    )
    ffn_pack = jnp.concatenate(
        [col_block[:, qkv_width:], row_pack[o_size:].reshape(block_rows, -1)], axis=1
    )
    y_stage, x_stage, z_stage = req_gather_stages(lax.axis_index("req"), REQ_DIMS)
    attn_y = y_stage(attn_pack)
    ffn_y = y_stage(ffn_pack)
    attn_x = x_stage(attn_y)
    ffn_z = z_stage(ffn_y)
    attn_x, ffn_z = lax.optimization_barrier((attn_x, ffn_z))
    attn_all = z_stage(attn_x)
    ffn_xz = x_stage(ffn_z)
    nz, nx, _ = REQ_DIMS
    ffn_all = (
        ffn_xz.reshape((nx, nz, -1) + ffn_xz.shape[1:])
        .transpose(1, 0, 2, 3)
        .reshape(ffn_xz.shape)
    )
    qkv_weight = attn_all[:, :qkv_width]
    out_weight = attn_all[:, qkv_width:].reshape(req_count, -1).reshape(-1, model_cols)

    prompt_batch, sequence_length, model_width = hidden_in.shape
    local_heads = q_cols // HEAD_DIM
    cosine_table, sine_table = rope_tables(sequence_length, HEAD_DIM)
    owner_shards = (
        tensor_shard_index * local_heads + jnp.arange(local_heads, dtype=jnp.int32)
    ) // (QUERY_HEADS // KEY_VALUE_HEADS)
    quarter_rows = sequence_length // tp_count
    row_start = (core_bit * 2 + chip_bit) * quarter_rows

    def attention(prompt_rows, length):
        flat_rows = prompt_rows.astype(jnp.float32)
        normalized_input = rms_norm(flat_rows, attn_gain)
        qkv = jnp.dot(normalized_input, qkv_weight, preferred_element_type=jnp.float32)
        queries = qkv[:, :q_cols].reshape(sequence_length, local_heads, HEAD_DIM)
        key_rows = qkv[:, q_cols : q_cols + kv_cols].reshape(
            sequence_length, KEY_VALUE_HEADS, HEAD_DIM
        )
        value_rows = qkv[:, q_cols + kv_cols :].reshape(sequence_length, KEY_VALUE_HEADS, HEAD_DIM)
        q_rot = rotate(queries, cosine_table, sine_table).astype(jnp.bfloat16)
        rotated_keys = rotate(key_rows, cosine_table, sine_table).astype(jnp.bfloat16)
        value_halves = value_rows.astype(jnp.bfloat16)
        cache = jnp.concatenate(
            [
                rotated_keys.reshape(sequence_length, KEY_VALUE_HEADS * HEAD_DIM),
                value_halves.reshape(sequence_length, KEY_VALUE_HEADS * HEAD_DIM),
            ],
            axis=1,
        )
        attended = causal_attention(
            q_rot.reshape(sequence_length, -1),
            jnp.take(rotated_keys, owner_shards, axis=1).reshape(sequence_length, -1),
            jnp.take(value_halves, owner_shards, axis=1).reshape(sequence_length, -1),
            length,
        )
        return flat_rows, attended, cache

    def finish(flat_rows, attended, gate_up_weight, down_weight):
        attn_partial = jnp.dot(attended, out_weight, preferred_element_type=jnp.float32).astype(bf)
        attn_mine = tp_reduce_scatter(attn_partial, core_bit, chip_bit)
        middle = lax.dynamic_slice_in_dim(flat_rows, row_start, quarter_rows, 0) + attn_mine
        normed_mine = rms_norm(middle, mlp_gain)
        from_cross = lax.ppermute(normed_mine, "tp", CROSS_PAIRS)
        half_rows = jnp.concatenate([normed_mine, from_cross], axis=0)
        from_chip = lax.ppermute(half_rows, "tp", CHIP_PAIRS)
        normed_rows = jnp.concatenate([half_rows, from_chip], axis=0)
        gate_up = jnp.dot(normed_rows, gate_up_weight, preferred_element_type=jnp.float32)
        gate_val = gate_up[:, :ff_cols]
        up_val = gate_up[:, ff_cols:]
        hidden_ff = (jax.nn.silu(gate_val) * up_val).astype(jnp.bfloat16)
        ffn_partial = jnp.dot(hidden_ff, down_weight, preferred_element_type=jnp.float32).astype(bf)
        half = 2 * quarter_rows
        got = lax.ppermute(ffn_partial[half:], "tp", CHIP_PAIRS)
        first = ffn_partial[:half].astype(jnp.float32) + got.astype(jnp.float32)
        got = lax.ppermute(first[quarter_rows:].astype(bf), "tp", CROSS_PAIRS)
        ffn_mine = first[:quarter_rows] + got.astype(jnp.float32)
        result_mine = (middle + ffn_mine).astype(jnp.bfloat16)
        return tp_all_gather(result_mine, core_bit, chip_bit)

    firsts = [attention(hidden_in[p], lengths[p]) for p in range(prompt_batch)]
    first_attended, ffn_all = lax.optimization_barrier((firsts[0][1], ffn_all))
    gate_up_weight = ffn_all[:, : 2 * ff_cols]
    down_weight = ffn_all[:, 2 * ff_cols :].reshape(req_count, -1).reshape(-1, model_cols)
    results = []
    for p, (flat_rows, attended, _) in enumerate(firsts):
        if p == 0:
            attended = first_attended
        results.append(finish(flat_rows, attended, gate_up_weight, down_weight))
    hidden_out = jnp.stack(results)
    kv_cache = jnp.stack([cache for _, _, cache in firsts])
    return (hidden_out, kv_cache)


def solution(mesh):
    placed = (
        P("req", None, None),
        P("req"),
        P(),
        P(),
        P(("req", "tp"), None),
        P(("req", "tp"), None),
        P(("req", "tp"), None),
        P(("req", "tp"), None),
        P(("req", "tp"), None),
        P(("req", "tp"), None),
        P(("req", "tp"), None),
    )
    return jax.shard_map(
        local,
        mesh=mesh,
        in_specs=placed,
        out_specs=(P("req", None, None), P("req", None, None)),
        check_vma=False,
    )
```

```python
import math

import jax
import jax.numpy as jnp
from jax import lax
from jax.experimental import pallas as pl
from jax.experimental.pallas import tpu as pltpu
from jax.sharding import PartitionSpec as P

QUERY_HEADS = 20
KEY_VALUE_HEADS = 5
HEAD_DIM = 64


def rms_norm(field, gain_vec):
    scale = lax.rsqrt(jnp.mean(field * field, axis=-1, keepdims=True) + 1e-05)
    return (field * scale * gain_vec).astype(jnp.bfloat16)


def rope_tables(sequence_length, head_size):
    half_width = head_size // 2
    positions = jnp.arange(sequence_length, dtype=jnp.float32)[:, None]
    frequency = jnp.exp(
        -math.log(10000.0) * (2.0 * jnp.arange(half_width, dtype=jnp.float32) / head_size)
    )
    angles = positions * frequency[None, :]
    return (jnp.cos(angles), jnp.sin(angles))


def rotate(field, cosine_table, sine_table):
    half_width = field.shape[-1] // 2
    first_half = field[..., :half_width]
    second_half = field[..., half_width:]
    cos_b = cosine_table[:, None, :]
    sin_b = sine_table[:, None, :]
    return jnp.concatenate(
        [first_half * cos_b - second_half * sin_b, second_half * cos_b + first_half * sin_b],
        axis=-1,
    )


REQ_DIMS = (4, 4, 2)
CHIP_PAIRS = [(0, 1), (1, 0), (2, 3), (3, 2)]
CROSS_PAIRS = [(0, 2), (2, 0), (1, 3), (3, 1)]


def _attn_body(len_ref, q_ref, k_ref, v_ref, o_ref):
    n = q_ref.shape[0]
    row = lax.broadcasted_iota(jnp.int32, (n, n), 0)
    col = lax.broadcasted_iota(jnp.int32, (n, n), 1)
    allowed = (col <= row) & (col < len_ref[0])
    for h in range(q_ref.shape[1] // HEAD_DIM):
        cols = slice(h * HEAD_DIM, (h + 1) * HEAD_DIM)
        q = q_ref[:, cols]
        k = k_ref[:, cols]
        v = v_ref[:, cols]
        s = lax.dot_general(q, k, (((1,), (1,)), ((), ())), preferred_element_type=jnp.float32) / 8.0
        s = jnp.where(allowed, s, -1e30)
        m = jnp.max(s, axis=-1, keepdims=True)
        e = jnp.exp(s - m)
        w = (e / jnp.sum(e, axis=-1, keepdims=True)).astype(jnp.bfloat16)
        o_ref[:, cols] = jnp.dot(w, v, preferred_element_type=jnp.float32).astype(o_ref.dtype)


def causal_attention(q, k, v, length, interpret=False):
    n, width = q.shape
    full = pl.BlockSpec((n, width), lambda i, ln: (0, 0))
    return pl.pallas_call(
        _attn_body,
        grid_spec=pltpu.PrefetchScalarGridSpec(
            num_scalar_prefetch=1, grid=(1,), in_specs=[full, full, full], out_specs=full
        ),
        out_shape=jax.ShapeDtypeStruct((n, width), jnp.bfloat16),
        interpret=interpret,
    )(length.reshape(1), q, k, v)


def pick(stack, index):
    return lax.dynamic_index_in_dim(stack, index, axis=0, keepdims=False)


def tp_reduce_scatter(partial, core_bit, chip_bit):
    rows, width = partial.shape
    halves = partial.reshape(2, rows // 2, width)
    got = lax.ppermute(pick(halves, 1 - core_bit), "tp", CHIP_PAIRS)
    first = pick(halves, core_bit).astype(jnp.float32) + got.astype(jnp.float32)
    quarters = first.reshape(2, rows // 4, width)
    sent = pick(quarters, 1 - chip_bit).astype(jnp.bfloat16)
    got = lax.ppermute(sent, "tp", CROSS_PAIRS)
    return pick(quarters, chip_bit) + got.astype(jnp.float32)


def tp_all_gather(quarter, core_bit, chip_bit):
    got = lax.ppermute(quarter, "tp", CROSS_PAIRS)
    half = jnp.zeros((2,) + quarter.shape, quarter.dtype)
    half = lax.dynamic_update_index_in_dim(half, quarter, chip_bit, 0)
    half = lax.dynamic_update_index_in_dim(half, got, 1 - chip_bit, 0)
    half = half.reshape((-1,) + quarter.shape[1:])
    got = lax.ppermute(half, "tp", CHIP_PAIRS)
    full = jnp.zeros((2,) + half.shape, half.dtype)
    full = lax.dynamic_update_index_in_dim(full, half, core_bit, 0)
    full = lax.dynamic_update_index_in_dim(full, got, 1 - core_bit, 0)
    return full.reshape((-1,) + half.shape[1:])


def ring_step(block, pos, size, shift_pairs):
    up, down = shift_pairs
    buf = jnp.zeros((size,) + block.shape, block.dtype)
    buf = lax.dynamic_update_index_in_dim(buf, block, pos, 0)
    from_below = lax.ppermute(block, "req", up)
    from_above = lax.ppermute(block, "req", down)
    buf = lax.dynamic_update_index_in_dim(buf, from_below, (pos + size - 1) % size, 0)
    buf = lax.dynamic_update_index_in_dim(buf, from_above, (pos + 1) % size, 0)
    half = block.shape[0] // 2
    far_low = lax.ppermute(from_below[:half], "req", up)
    far_high = lax.ppermute(from_above[half:], "req", down)
    far = jnp.concatenate([far_low, far_high], axis=0)
    buf = lax.dynamic_update_index_in_dim(buf, far, (pos + 2) % size, 0)
    return buf.reshape((size * block.shape[0],) + block.shape[1:])


def req_gather_stages(req_index, dims):
    nz, nx, ny = dims
    z = req_index // (nx * ny)
    x = (req_index // ny) % nx
    y = req_index % ny
    ids = [(a, b, c) for a in range(nz) for b in range(nx) for c in range(ny)]

    def lin(a, b, c):
        return (a * nx + b) * ny + c

    y_pairs = [(lin(a, b, c), lin(a, b, 1 - c)) for a, b, c in ids]
    x_pairs = (
        [(lin(a, b, c), lin(a, (b + 1) % nx, c)) for a, b, c in ids],
        [(lin(a, b, c), lin(a, (b - 1) % nx, c)) for a, b, c in ids],
    )
    z_pairs = (
        [(lin(a, b, c), lin((a + 1) % nz, b, c)) for a, b, c in ids],
        [(lin(a, b, c), lin((a - 1) % nz, b, c)) for a, b, c in ids],
    )

    def y_stage(block):
        got = lax.ppermute(block, "req", y_pairs)
        return jnp.where(
            y == 0, jnp.concatenate([block, got], 0), jnp.concatenate([got, block], 0)
        )

    def x_stage(block):
        return ring_step(block, x, nx, x_pairs)

    def z_stage(block):
        return ring_step(block, z, nz, z_pairs)

    return y_stage, x_stage, z_stage


def local(
    hidden_in,
    lengths,
    attn_gain,
    mlp_gain,
    q_master,
    k_master,
    trainer_value_weight,
    o_master,
    gate_master,
    up_master,
    down_master,
):
    tp_count = lax.axis_size("tp")
    req_count = lax.axis_size("req")
    tensor_shard_index = lax.axis_index("tp")
    core_bit = tensor_shard_index % 2
    chip_bit = tensor_shard_index // 2
    bf = jnp.bfloat16
    q_cols = q_master.shape[1] // tp_count
    kv_cols = k_master.shape[1]
    ff_cols = gate_master.shape[1] // tp_count
    local_rows = q_master.shape[0]
    model_cols = o_master.shape[1]
    block_rows = tp_count * local_rows

    def attn_chunk(dest):
        return jnp.concatenate(
            [q_master[:, dest * q_cols : (dest + 1) * q_cols], k_master, trainer_value_weight],
            axis=1,
        ).astype(bf)

    def ffn_chunk(dest):
        return jnp.concatenate(
            [
                gate_master[:, dest * ff_cols : (dest + 1) * ff_cols],
                up_master[:, dest * ff_cols : (dest + 1) * ff_cols],
            ],
            axis=1,
        ).astype(bf)

    attn_cols = lax.all_to_all(
        jnp.stack([attn_chunk(d) for d in range(tp_count)]), "tp", 0, 0, tiled=False
    ).reshape(block_rows, -1)
    ffn_cols = lax.all_to_all(
        jnp.stack([ffn_chunk(d) for d in range(tp_count)]), "tp", 0, 0, tiled=False
    ).reshape(block_rows, -1)
    qkv_width = q_cols + 2 * kv_cols

    o_size = o_master.size
    row_pack = jnp.concatenate([o_master.reshape(-1), down_master.reshape(-1)]).astype(bf)
    per_block = req_count // tp_count
    perm = []
    for r_src in range(req_count):
        for t_src in range(tp_count):
            r_dst = tp_count * (r_src % per_block) + t_src
            t_dst = r_src // per_block
            perm.append((r_src * tp_count + t_src, r_dst * tp_count + t_dst))
    row_pack = lax.ppermute(row_pack, ("req", "tp"), perm)

    attn_pack = jnp.concatenate(
        [attn_cols, row_pack[:o_size].reshape(block_rows, -1)], axis=1
    )
    ffn_pack = jnp.concatenate(
        [ffn_cols, row_pack[o_size:].reshape(block_rows, -1)], axis=1
    )
    y_stage, x_stage, z_stage = req_gather_stages(lax.axis_index("req"), REQ_DIMS)
    attn_y = y_stage(attn_pack)
    ffn_y = y_stage(ffn_pack)
    attn_x = x_stage(attn_y)
    ffn_z = z_stage(ffn_y)
    attn_x, ffn_z = lax.optimization_barrier((attn_x, ffn_z))
    attn_all = z_stage(attn_x)
    ffn_xz = x_stage(ffn_z)
    nz, nx, _ = REQ_DIMS
    ffn_all = (
        ffn_xz.reshape((nx, nz, -1) + ffn_xz.shape[1:])
        .transpose(1, 0, 2, 3)
        .reshape(ffn_xz.shape)
    )
    qkv_weight = attn_all[:, :qkv_width]
    out_weight = attn_all[:, qkv_width:].reshape(req_count, -1).reshape(-1, model_cols)

    prompt_batch, sequence_length, model_width = hidden_in.shape
    local_heads = q_cols // HEAD_DIM
    cosine_table, sine_table = rope_tables(sequence_length, HEAD_DIM)
    owner_shards = (
        tensor_shard_index * local_heads + jnp.arange(local_heads, dtype=jnp.int32)
    ) // (QUERY_HEADS // KEY_VALUE_HEADS)
    quarter_rows = sequence_length // tp_count
    row_start = (core_bit * 2 + chip_bit) * quarter_rows

    def attention(prompt_rows, length):
        flat_rows = prompt_rows.astype(jnp.float32)
        normalized_input = rms_norm(flat_rows, attn_gain)
        qkv = jnp.dot(normalized_input, qkv_weight, preferred_element_type=jnp.float32)
        queries = qkv[:, :q_cols].reshape(sequence_length, local_heads, HEAD_DIM)
        key_rows = qkv[:, q_cols : q_cols + kv_cols].reshape(
            sequence_length, KEY_VALUE_HEADS, HEAD_DIM
        )
        value_rows = qkv[:, q_cols + kv_cols :].reshape(sequence_length, KEY_VALUE_HEADS, HEAD_DIM)
        q_rot = rotate(queries, cosine_table, sine_table).astype(jnp.bfloat16)
        rotated_keys = rotate(key_rows, cosine_table, sine_table).astype(jnp.bfloat16)
        value_halves = value_rows.astype(jnp.bfloat16)
        cache = jnp.concatenate(
            [
                rotated_keys.reshape(sequence_length, KEY_VALUE_HEADS * HEAD_DIM),
                value_halves.reshape(sequence_length, KEY_VALUE_HEADS * HEAD_DIM),
            ],
            axis=1,
        )
        attended = causal_attention(
            q_rot.reshape(sequence_length, -1),
            jnp.take(rotated_keys, owner_shards, axis=1).reshape(sequence_length, -1),
            jnp.take(value_halves, owner_shards, axis=1).reshape(sequence_length, -1),
            length,
        )
        return flat_rows, attended, cache

    def finish(flat_rows, attended, gate_up_weight, down_weight):
        attn_partial = jnp.dot(attended, out_weight, preferred_element_type=jnp.float32).astype(bf)
        attn_mine = tp_reduce_scatter(attn_partial, core_bit, chip_bit)
        middle = lax.dynamic_slice_in_dim(flat_rows, row_start, quarter_rows, 0) + attn_mine
        normed_mine = rms_norm(middle, mlp_gain)
        normed_rows = tp_all_gather(normed_mine, core_bit, chip_bit)
        gate_up = jnp.dot(normed_rows, gate_up_weight, preferred_element_type=jnp.float32)
        gate_val = gate_up[:, :ff_cols]
        up_val = gate_up[:, ff_cols:]
        hidden_ff = (jax.nn.silu(gate_val) * up_val).astype(jnp.bfloat16)
        ffn_partial = jnp.dot(hidden_ff, down_weight, preferred_element_type=jnp.float32).astype(bf)
        ffn_mine = tp_reduce_scatter(ffn_partial, core_bit, chip_bit)
        result_mine = (middle + ffn_mine).astype(jnp.bfloat16)
        return tp_all_gather(result_mine, core_bit, chip_bit)

    firsts = [attention(hidden_in[p], lengths[p]) for p in range(prompt_batch)]
    first_attended, ffn_all = lax.optimization_barrier((firsts[0][1], ffn_all))
    gate_up_weight = ffn_all[:, : 2 * ff_cols]
    down_weight = ffn_all[:, 2 * ff_cols :].reshape(req_count, -1).reshape(-1, model_cols)
    results = []
    for p, (flat_rows, attended, _) in enumerate(firsts):
        if p == 0:
            attended = first_attended
        results.append(finish(flat_rows, attended, gate_up_weight, down_weight))
    hidden_out = jnp.stack(results)
    kv_cache = jnp.stack([cache for _, _, cache in firsts])
    return (hidden_out, kv_cache)


def solution(mesh):
    placed = (
        P("req", None, None),
        P("req"),
        P(),
        P(),
        P(("req", "tp"), None),
        P(("req", "tp"), None),
        P(("req", "tp"), None),
        P(("req", "tp"), None),
        P(("req", "tp"), None),
        P(("req", "tp"), None),
        P(("req", "tp"), None),
    )
    return jax.shard_map(
        local,
        mesh=mesh,
        in_specs=placed,
        out_specs=(P("req", None, None), P("req", None, None)),
        check_vma=False,
    )
```

```python
import math

import jax
import jax.numpy as jnp
from jax import lax
from jax.experimental import pallas as pl
from jax.experimental.pallas import tpu as pltpu
from jax.sharding import PartitionSpec as P

QUERY_HEADS = 20
KEY_VALUE_HEADS = 5
HEAD_DIM = 64


def rms_norm(field, gain_vec):
    scale = lax.rsqrt(jnp.mean(field * field, axis=-1, keepdims=True) + 1e-05)
    return (field * scale * gain_vec).astype(jnp.bfloat16)


def rope_tables(sequence_length, head_size):
    half_width = head_size // 2
    positions = jnp.arange(sequence_length, dtype=jnp.float32)[:, None]
    frequency = jnp.exp(
        -math.log(10000.0) * (2.0 * jnp.arange(half_width, dtype=jnp.float32) / head_size)
    )
    angles = positions * frequency[None, :]
    return (jnp.cos(angles), jnp.sin(angles))


def rotate(field, cosine_table, sine_table):
    half_width = field.shape[-1] // 2
    first_half = field[..., :half_width]
    second_half = field[..., half_width:]
    cos_b = cosine_table[:, None, :]
    sin_b = sine_table[:, None, :]
    return jnp.concatenate(
        [first_half * cos_b - second_half * sin_b, second_half * cos_b + first_half * sin_b],
        axis=-1,
    )


REQ_DIMS = (4, 4, 2)
CHIP_PAIRS = [(0, 1), (1, 0), (2, 3), (3, 2)]
CROSS_PAIRS = [(0, 2), (2, 0), (1, 3), (3, 1)]


def _attn_body(len_ref, q_ref, k_ref, v_ref, o_ref):
    n = q_ref.shape[0]
    row = lax.broadcasted_iota(jnp.int32, (n, n), 0)
    col = lax.broadcasted_iota(jnp.int32, (n, n), 1)
    allowed = (col <= row) & (col < len_ref[0])
    for h in range(q_ref.shape[1] // HEAD_DIM):
        cols = slice(h * HEAD_DIM, (h + 1) * HEAD_DIM)
        q = q_ref[:, cols]
        k = k_ref[:, cols]
        v = v_ref[:, cols]
        s = lax.dot_general(q, k, (((1,), (1,)), ((), ())), preferred_element_type=jnp.float32) / 8.0
        s = jnp.where(allowed, s, -1e30)
        m = jnp.max(s, axis=-1, keepdims=True)
        e = jnp.exp(s - m)
        w = (e / jnp.sum(e, axis=-1, keepdims=True)).astype(jnp.bfloat16)
        o_ref[:, cols] = jnp.dot(w, v, preferred_element_type=jnp.float32).astype(o_ref.dtype)


def causal_attention(q, k, v, length, interpret=False):
    n, width = q.shape
    full = pl.BlockSpec((n, width), lambda i, ln: (0, 0))
    return pl.pallas_call(
        _attn_body,
        grid_spec=pltpu.PrefetchScalarGridSpec(
            num_scalar_prefetch=1, grid=(1,), in_specs=[full, full, full], out_specs=full
        ),
        out_shape=jax.ShapeDtypeStruct((n, width), jnp.bfloat16),
        interpret=interpret,
    )(length.reshape(1), q, k, v)


def pick(stack, index):
    return lax.dynamic_index_in_dim(stack, index, axis=0, keepdims=False)


def tp_reduce_scatter(partial, core_bit, chip_bit):
    rows, width = partial.shape
    halves = partial.reshape(2, rows // 2, width)
    got = lax.ppermute(pick(halves, 1 - core_bit), "tp", CHIP_PAIRS)
    first = pick(halves, core_bit).astype(jnp.float32) + got.astype(jnp.float32)
    quarters = first.reshape(2, rows // 4, width)
    sent = pick(quarters, 1 - chip_bit).astype(jnp.bfloat16)
    got = lax.ppermute(sent, "tp", CROSS_PAIRS)
    return pick(quarters, chip_bit) + got.astype(jnp.float32)


def tp_all_gather(quarter, core_bit, chip_bit):
    got = lax.ppermute(quarter, "tp", CROSS_PAIRS)
    half = jnp.zeros((2,) + quarter.shape, quarter.dtype)
    half = lax.dynamic_update_index_in_dim(half, quarter, chip_bit, 0)
    half = lax.dynamic_update_index_in_dim(half, got, 1 - chip_bit, 0)
    half = half.reshape((-1,) + quarter.shape[1:])
    got = lax.ppermute(half, "tp", CHIP_PAIRS)
    full = jnp.zeros((2,) + half.shape, half.dtype)
    full = lax.dynamic_update_index_in_dim(full, half, core_bit, 0)
    full = lax.dynamic_update_index_in_dim(full, got, 1 - core_bit, 0)
    return full.reshape((-1,) + half.shape[1:])


def ring_step(block, pos, size, shift_pairs):
    up, down = shift_pairs
    buf = jnp.zeros((size,) + block.shape, block.dtype)
    buf = lax.dynamic_update_index_in_dim(buf, block, pos, 0)
    from_below = lax.ppermute(block, "req", up)
    from_above = lax.ppermute(block, "req", down)
    buf = lax.dynamic_update_index_in_dim(buf, from_below, (pos + size - 1) % size, 0)
    buf = lax.dynamic_update_index_in_dim(buf, from_above, (pos + 1) % size, 0)
    half = block.shape[0] // 2
    far_low = lax.ppermute(from_below[:half], "req", up)
    far_high = lax.ppermute(from_above[half:], "req", down)
    far = jnp.concatenate([far_low, far_high], axis=0)
    buf = lax.dynamic_update_index_in_dim(buf, far, (pos + 2) % size, 0)
    return buf.reshape((size * block.shape[0],) + block.shape[1:])


def req_gather_stages(req_index, dims):
    nz, nx, ny = dims
    z = req_index // (nx * ny)
    x = (req_index // ny) % nx
    y = req_index % ny
    ids = [(a, b, c) for a in range(nz) for b in range(nx) for c in range(ny)]

    def lin(a, b, c):
        return (a * nx + b) * ny + c

    y_pairs = [(lin(a, b, c), lin(a, b, 1 - c)) for a, b, c in ids]
    x_pairs = (
        [(lin(a, b, c), lin(a, (b + 1) % nx, c)) for a, b, c in ids],
        [(lin(a, b, c), lin(a, (b - 1) % nx, c)) for a, b, c in ids],
    )
    z_pairs = (
        [(lin(a, b, c), lin((a + 1) % nz, b, c)) for a, b, c in ids],
        [(lin(a, b, c), lin((a - 1) % nz, b, c)) for a, b, c in ids],
    )

    def y_stage(block):
        got = lax.ppermute(block, "req", y_pairs)
        return jnp.where(
            y == 0, jnp.concatenate([block, got], 0), jnp.concatenate([got, block], 0)
        )

    def x_stage(block):
        return ring_step(block, x, nx, x_pairs)

    def z_stage(block):
        return ring_step(block, z, nz, z_pairs)

    return y_stage, x_stage, z_stage


def local(
    hidden_in,
    lengths,
    attn_gain,
    mlp_gain,
    q_master,
    k_master,
    trainer_value_weight,
    o_master,
    gate_master,
    up_master,
    down_master,
):
    tp_count = lax.axis_size("tp")
    req_count = lax.axis_size("req")
    tensor_shard_index = lax.axis_index("tp")
    core_bit = tensor_shard_index % 2
    chip_bit = tensor_shard_index // 2
    bf = jnp.bfloat16
    q_cols = q_master.shape[1] // tp_count
    kv_cols = k_master.shape[1]
    ff_cols = gate_master.shape[1] // tp_count
    local_rows = q_master.shape[0]
    model_cols = o_master.shape[1]
    block_rows = tp_count * local_rows

    def dest_chunk(dest):
        return jnp.concatenate(
            [
                q_master[:, dest * q_cols : (dest + 1) * q_cols],
                k_master,
                trainer_value_weight,
                gate_master[:, dest * ff_cols : (dest + 1) * ff_cols],
                up_master[:, dest * ff_cols : (dest + 1) * ff_cols],
            ],
            axis=1,
        ).astype(bf)

    send = jnp.stack([dest_chunk(d) for d in range(tp_count)])
    recv = lax.all_to_all(send, "tp", 0, 0, tiled=False)
    col_block = recv.reshape(block_rows, -1)
    qkv_width = q_cols + 2 * kv_cols

    o_size = o_master.size
    row_pack = jnp.concatenate([o_master.reshape(-1), down_master.reshape(-1)]).astype(bf)
    per_block = req_count // tp_count
    perm = []
    for r_src in range(req_count):
        for t_src in range(tp_count):
            r_dst = tp_count * (r_src % per_block) + t_src
            t_dst = r_src // per_block
            perm.append((r_src * tp_count + t_src, r_dst * tp_count + t_dst))
    row_pack = lax.ppermute(row_pack, ("req", "tp"), perm)

    attn_pack = jnp.concatenate(
        [col_block[:, :qkv_width], row_pack[:o_size].reshape(block_rows, -1)], axis=1
    )
    ffn_pack = jnp.concatenate(
        [col_block[:, qkv_width:], row_pack[o_size:].reshape(block_rows, -1)], axis=1
    )
    y_stage, x_stage, z_stage = req_gather_stages(lax.axis_index("req"), REQ_DIMS)
    attn_y = y_stage(attn_pack)
    ffn_y = y_stage(ffn_pack)
    attn_x = x_stage(attn_y)
    ffn_z = z_stage(ffn_y)
    attn_x, ffn_z = lax.optimization_barrier((attn_x, ffn_z))
    attn_all = z_stage(attn_x)
    ffn_xz = x_stage(ffn_z)
    nz, nx, _ = REQ_DIMS
    ffn_all = (
        ffn_xz.reshape((nx, nz, -1) + ffn_xz.shape[1:])
        .transpose(1, 0, 2, 3)
        .reshape(ffn_xz.shape)
    )
    qkv_weight = attn_all[:, :qkv_width]
    out_weight = attn_all[:, qkv_width:].reshape(req_count, -1).reshape(-1, model_cols)

    prompt_batch, sequence_length, model_width = hidden_in.shape
    local_heads = q_cols // HEAD_DIM
    cosine_table, sine_table = rope_tables(sequence_length, HEAD_DIM)
    owner_shards = (
        tensor_shard_index * local_heads + jnp.arange(local_heads, dtype=jnp.int32)
    ) // (QUERY_HEADS // KEY_VALUE_HEADS)
    quarter_rows = sequence_length // tp_count
    row_start = (core_bit * 2 + chip_bit) * quarter_rows

    def attention(prompt_rows, length):
        flat_rows = prompt_rows.astype(jnp.float32)
        normalized_input = rms_norm(flat_rows, attn_gain)
        qkv = jnp.dot(normalized_input, qkv_weight, preferred_element_type=jnp.float32)
        queries = qkv[:, :q_cols].reshape(sequence_length, local_heads, HEAD_DIM)
        key_rows = qkv[:, q_cols : q_cols + kv_cols].reshape(
            sequence_length, KEY_VALUE_HEADS, HEAD_DIM
        )
        value_rows = qkv[:, q_cols + kv_cols :].reshape(sequence_length, KEY_VALUE_HEADS, HEAD_DIM)
        q_rot = rotate(queries, cosine_table, sine_table).astype(jnp.bfloat16)
        rotated_keys = rotate(key_rows, cosine_table, sine_table).astype(jnp.bfloat16)
        value_halves = value_rows.astype(jnp.bfloat16)
        cache = jnp.concatenate(
            [
                rotated_keys.reshape(sequence_length, KEY_VALUE_HEADS * HEAD_DIM),
                value_halves.reshape(sequence_length, KEY_VALUE_HEADS * HEAD_DIM),
            ],
            axis=1,
        )
        attended = causal_attention(
            q_rot.reshape(sequence_length, -1),
            jnp.take(rotated_keys, owner_shards, axis=1).reshape(sequence_length, -1),
            jnp.take(value_halves, owner_shards, axis=1).reshape(sequence_length, -1),
            length,
        )
        return flat_rows, attended, cache

    def finish(flat_rows, attended, gate_up_weight, down_weight):
        attn_partial = jnp.dot(attended, out_weight, preferred_element_type=jnp.float32).astype(bf)
        attn_mine = tp_reduce_scatter(attn_partial, core_bit, chip_bit)
        middle = lax.dynamic_slice_in_dim(flat_rows, row_start, quarter_rows, 0) + attn_mine
        normed_mine = rms_norm(middle, mlp_gain)
        normed_rows = tp_all_gather(normed_mine, core_bit, chip_bit)
        gate_up = jnp.dot(normed_rows, gate_up_weight, preferred_element_type=jnp.float32)
        gate_val = gate_up[:, :ff_cols]
        up_val = gate_up[:, ff_cols:]
        hidden_ff = (jax.nn.silu(gate_val) * up_val).astype(jnp.bfloat16)
        ffn_partial = jnp.dot(hidden_ff, down_weight, preferred_element_type=jnp.float32).astype(bf)
        ffn_mine = tp_reduce_scatter(ffn_partial, core_bit, chip_bit)
        result_mine = (middle + ffn_mine).astype(jnp.bfloat16)
        return tp_all_gather(result_mine, core_bit, chip_bit)

    firsts = [attention(hidden_in[p], lengths[p]) for p in range(prompt_batch)]
    first_attended = firsts[0][1]
    gate_up_weight = ffn_all[:, : 2 * ff_cols]
    down_weight = ffn_all[:, 2 * ff_cols :].reshape(req_count, -1).reshape(-1, model_cols)
    results = []
    for p, (flat_rows, attended, _) in enumerate(firsts):
        if p == 0:
            attended = first_attended
        results.append(finish(flat_rows, attended, gate_up_weight, down_weight))
    hidden_out = jnp.stack(results)
    kv_cache = jnp.stack([cache for _, _, cache in firsts])
    return (hidden_out, kv_cache)


def solution(mesh):
    placed = (
        P("req", None, None),
        P("req"),
        P(),
        P(),
        P(("req", "tp"), None),
        P(("req", "tp"), None),
        P(("req", "tp"), None),
        P(("req", "tp"), None),
        P(("req", "tp"), None),
        P(("req", "tp"), None),
        P(("req", "tp"), None),
    )
    return jax.shard_map(
        local,
        mesh=mesh,
        in_specs=placed,
        out_specs=(P("req", None, None), P("req", None, None)),
        check_vma=False,
    )
```

```python
import math

import jax
import jax.numpy as jnp
from jax import lax
from jax.experimental import pallas as pl
from jax.experimental.pallas import tpu as pltpu
from jax.sharding import PartitionSpec as P

QUERY_HEADS = 20
KEY_VALUE_HEADS = 5
HEAD_DIM = 64


def rms_norm(field, gain_vec):
    scale = lax.rsqrt(jnp.mean(field * field, axis=-1, keepdims=True) + 1e-05)
    return (field * scale * gain_vec).astype(jnp.bfloat16)


def rope_tables(sequence_length, head_size):
    half_width = head_size // 2
    positions = jnp.arange(sequence_length, dtype=jnp.float32)[:, None]
    frequency = jnp.exp(
        -math.log(10000.0) * (2.0 * jnp.arange(half_width, dtype=jnp.float32) / head_size)
    )
    angles = positions * frequency[None, :]
    return (jnp.cos(angles), jnp.sin(angles))


def rotate(field, cosine_table, sine_table):
    half_width = field.shape[-1] // 2
    first_half = field[..., :half_width]
    second_half = field[..., half_width:]
    cos_b = cosine_table[:, None, :]
    sin_b = sine_table[:, None, :]
    return jnp.concatenate(
        [first_half * cos_b - second_half * sin_b, second_half * cos_b + first_half * sin_b],
        axis=-1,
    )


REQ_DIMS = (4, 4, 2)
CHIP_PAIRS = [(0, 1), (1, 0), (2, 3), (3, 2)]
CROSS_PAIRS = [(0, 2), (2, 0), (1, 3), (3, 1)]


def _attn_body(len_ref, q_ref, k_ref, v_ref, o_ref):
    n = q_ref.shape[0]
    row = lax.broadcasted_iota(jnp.int32, (n, n), 0)
    col = lax.broadcasted_iota(jnp.int32, (n, n), 1)
    allowed = (col <= row) & (col < len_ref[0])
    for h in range(q_ref.shape[1] // HEAD_DIM):
        cols = slice(h * HEAD_DIM, (h + 1) * HEAD_DIM)
        q = q_ref[:, cols]
        k = k_ref[:, cols]
        v = v_ref[:, cols]
        s = lax.dot_general(q, k, (((1,), (1,)), ((), ())), preferred_element_type=jnp.float32) / 8.0
        s = jnp.where(allowed, s, -1e30)
        m = jnp.max(s, axis=-1, keepdims=True)
        e = jnp.exp(s - m)
        w = (e / jnp.sum(e, axis=-1, keepdims=True)).astype(jnp.bfloat16)
        o_ref[:, cols] = jnp.dot(w, v, preferred_element_type=jnp.float32).astype(o_ref.dtype)


def causal_attention(q, k, v, length, interpret=False):
    n, width = q.shape
    full = pl.BlockSpec((n, width), lambda i, ln: (0, 0))
    return pl.pallas_call(
        _attn_body,
        grid_spec=pltpu.PrefetchScalarGridSpec(
            num_scalar_prefetch=1, grid=(1,), in_specs=[full, full, full], out_specs=full
        ),
        out_shape=jax.ShapeDtypeStruct((n, width), jnp.bfloat16),
        cost_estimate=pl.CostEstimate(
            flops=4 * n * n * width,
            transcendentals=n * n * (width // HEAD_DIM),
            bytes_accessed=4 * n * width * 2,
        ),
        interpret=interpret,
    )(length.reshape(1), q, k, v)


def pick(stack, index):
    return lax.dynamic_index_in_dim(stack, index, axis=0, keepdims=False)


def tp_reduce_scatter(partial, core_bit, chip_bit):
    rows, width = partial.shape
    halves = partial.reshape(2, rows // 2, width)
    got = lax.ppermute(pick(halves, 1 - core_bit), "tp", CHIP_PAIRS)
    first = pick(halves, core_bit).astype(jnp.float32) + got.astype(jnp.float32)
    quarters = first.reshape(2, rows // 4, width)
    sent = pick(quarters, 1 - chip_bit).astype(jnp.bfloat16)
    got = lax.ppermute(sent, "tp", CROSS_PAIRS)
    return pick(quarters, chip_bit) + got.astype(jnp.float32)


def tp_all_gather(quarter, core_bit, chip_bit):
    got = lax.ppermute(quarter, "tp", CROSS_PAIRS)
    half = jnp.zeros((2,) + quarter.shape, quarter.dtype)
    half = lax.dynamic_update_index_in_dim(half, quarter, chip_bit, 0)
    half = lax.dynamic_update_index_in_dim(half, got, 1 - chip_bit, 0)
    half = half.reshape((-1,) + quarter.shape[1:])
    got = lax.ppermute(half, "tp", CHIP_PAIRS)
    full = jnp.zeros((2,) + half.shape, half.dtype)
    full = lax.dynamic_update_index_in_dim(full, half, core_bit, 0)
    full = lax.dynamic_update_index_in_dim(full, got, 1 - core_bit, 0)
    return full.reshape((-1,) + half.shape[1:])


def ring_step(block, pos, size, shift_pairs):
    up, down = shift_pairs
    buf = jnp.zeros((size,) + block.shape, block.dtype)
    buf = lax.dynamic_update_index_in_dim(buf, block, pos, 0)
    from_below = lax.ppermute(block, "req", up)
    from_above = lax.ppermute(block, "req", down)
    buf = lax.dynamic_update_index_in_dim(buf, from_below, (pos + size - 1) % size, 0)
    buf = lax.dynamic_update_index_in_dim(buf, from_above, (pos + 1) % size, 0)
    half = block.shape[0] // 2
    far_low = lax.ppermute(from_below[:half], "req", up)
    far_high = lax.ppermute(from_above[half:], "req", down)
    far = jnp.concatenate([far_low, far_high], axis=0)
    buf = lax.dynamic_update_index_in_dim(buf, far, (pos + 2) % size, 0)
    return buf.reshape((size * block.shape[0],) + block.shape[1:])


def req_gather_stages(req_index, dims):
    nz, nx, ny = dims
    z = req_index // (nx * ny)
    x = (req_index // ny) % nx
    y = req_index % ny
    ids = [(a, b, c) for a in range(nz) for b in range(nx) for c in range(ny)]

    def lin(a, b, c):
        return (a * nx + b) * ny + c

    y_pairs = [(lin(a, b, c), lin(a, b, 1 - c)) for a, b, c in ids]
    x_pairs = (
        [(lin(a, b, c), lin(a, (b + 1) % nx, c)) for a, b, c in ids],
        [(lin(a, b, c), lin(a, (b - 1) % nx, c)) for a, b, c in ids],
    )
    z_pairs = (
        [(lin(a, b, c), lin((a + 1) % nz, b, c)) for a, b, c in ids],
        [(lin(a, b, c), lin((a - 1) % nz, b, c)) for a, b, c in ids],
    )

    def y_stage(block):
        got = lax.ppermute(block, "req", y_pairs)
        return jnp.where(
            y == 0, jnp.concatenate([block, got], 0), jnp.concatenate([got, block], 0)
        )

    def x_stage(block):
        return ring_step(block, x, nx, x_pairs)

    def z_stage(block):
        return ring_step(block, z, nz, z_pairs)

    return y_stage, x_stage, z_stage


def local(
    hidden_in,
    lengths,
    attn_gain,
    mlp_gain,
    q_master,
    k_master,
    trainer_value_weight,
    o_master,
    gate_master,
    up_master,
    down_master,
):
    tp_count = lax.axis_size("tp")
    req_count = lax.axis_size("req")
    tensor_shard_index = lax.axis_index("tp")
    core_bit = tensor_shard_index % 2
    chip_bit = tensor_shard_index // 2
    bf = jnp.bfloat16
    q_cols = q_master.shape[1] // tp_count
    kv_cols = k_master.shape[1]
    ff_cols = gate_master.shape[1] // tp_count
    local_rows = q_master.shape[0]
    model_cols = o_master.shape[1]
    block_rows = tp_count * local_rows

    def dest_chunk(dest):
        return jnp.concatenate(
            [
                q_master[:, dest * q_cols : (dest + 1) * q_cols],
                k_master,
                trainer_value_weight,
                gate_master[:, dest * ff_cols : (dest + 1) * ff_cols],
                up_master[:, dest * ff_cols : (dest + 1) * ff_cols],
            ],
            axis=1,
        ).astype(bf)

    send = jnp.stack([dest_chunk(d) for d in range(tp_count)])
    recv = lax.all_to_all(send, "tp", 0, 0, tiled=False)
    col_block = recv.reshape(block_rows, -1)
    qkv_width = q_cols + 2 * kv_cols

    o_size = o_master.size
    row_pack = jnp.concatenate([o_master.reshape(-1), down_master.reshape(-1)]).astype(bf)
    per_block = req_count // tp_count
    perm = []
    for r_src in range(req_count):
        for t_src in range(tp_count):
            r_dst = tp_count * (r_src % per_block) + t_src
            t_dst = r_src // per_block
            perm.append((r_src * tp_count + t_src, r_dst * tp_count + t_dst))
    row_pack = lax.ppermute(row_pack, ("req", "tp"), perm)

    attn_pack = jnp.concatenate(
        [col_block[:, :qkv_width], row_pack[:o_size].reshape(block_rows, -1)], axis=1
    )
    ffn_pack = jnp.concatenate(
        [col_block[:, qkv_width:], row_pack[o_size:].reshape(block_rows, -1)], axis=1
    )
    y_stage, x_stage, z_stage = req_gather_stages(lax.axis_index("req"), REQ_DIMS)
    attn_y = y_stage(attn_pack)
    ffn_y = y_stage(ffn_pack)
    attn_x = x_stage(attn_y)
    ffn_z = z_stage(ffn_y)
    attn_x, ffn_z = lax.optimization_barrier((attn_x, ffn_z))
    attn_all = z_stage(attn_x)
    ffn_xz = x_stage(ffn_z)
    nz, nx, _ = REQ_DIMS
    ffn_all = (
        ffn_xz.reshape((nx, nz, -1) + ffn_xz.shape[1:])
        .transpose(1, 0, 2, 3)
        .reshape(ffn_xz.shape)
    )
    qkv_weight = attn_all[:, :qkv_width]
    out_weight = attn_all[:, qkv_width:].reshape(req_count, -1).reshape(-1, model_cols)

    prompt_batch, sequence_length, model_width = hidden_in.shape
    local_heads = q_cols // HEAD_DIM
    cosine_table, sine_table = rope_tables(sequence_length, HEAD_DIM)
    owner_shards = (
        tensor_shard_index * local_heads + jnp.arange(local_heads, dtype=jnp.int32)
    ) // (QUERY_HEADS // KEY_VALUE_HEADS)
    quarter_rows = sequence_length // tp_count
    row_start = (core_bit * 2 + chip_bit) * quarter_rows

    def attention(prompt_rows, length):
        flat_rows = prompt_rows.astype(jnp.float32)
        normalized_input = rms_norm(flat_rows, attn_gain)
        qkv = jnp.dot(normalized_input, qkv_weight, preferred_element_type=jnp.float32)
        queries = qkv[:, :q_cols].reshape(sequence_length, local_heads, HEAD_DIM)
        key_rows = qkv[:, q_cols : q_cols + kv_cols].reshape(
            sequence_length, KEY_VALUE_HEADS, HEAD_DIM
        )
        value_rows = qkv[:, q_cols + kv_cols :].reshape(sequence_length, KEY_VALUE_HEADS, HEAD_DIM)
        q_rot = rotate(queries, cosine_table, sine_table).astype(jnp.bfloat16)
        rotated_keys = rotate(key_rows, cosine_table, sine_table).astype(jnp.bfloat16)
        value_halves = value_rows.astype(jnp.bfloat16)
        cache = jnp.concatenate(
            [
                rotated_keys.reshape(sequence_length, KEY_VALUE_HEADS * HEAD_DIM),
                value_halves.reshape(sequence_length, KEY_VALUE_HEADS * HEAD_DIM),
            ],
            axis=1,
        )
        attended = causal_attention(
            q_rot.reshape(sequence_length, -1),
            jnp.take(rotated_keys, owner_shards, axis=1).reshape(sequence_length, -1),
            jnp.take(value_halves, owner_shards, axis=1).reshape(sequence_length, -1),
            length,
        )
        return flat_rows, attended, cache

    def finish(flat_rows, attended, gate_up_weight, down_weight):
        attn_partial = jnp.dot(attended, out_weight, preferred_element_type=jnp.float32).astype(bf)
        attn_mine = tp_reduce_scatter(attn_partial, core_bit, chip_bit)
        middle = lax.dynamic_slice_in_dim(flat_rows, row_start, quarter_rows, 0) + attn_mine
        normed_mine = rms_norm(middle, mlp_gain)
        normed_rows = tp_all_gather(normed_mine, core_bit, chip_bit)
        gate_up = jnp.dot(normed_rows, gate_up_weight, preferred_element_type=jnp.float32)
        gate_val = gate_up[:, :ff_cols]
        up_val = gate_up[:, ff_cols:]
        hidden_ff = (jax.nn.silu(gate_val) * up_val).astype(jnp.bfloat16)
        ffn_partial = jnp.dot(hidden_ff, down_weight, preferred_element_type=jnp.float32).astype(bf)
        ffn_mine = tp_reduce_scatter(ffn_partial, core_bit, chip_bit)
        result_mine = (middle + ffn_mine).astype(jnp.bfloat16)
        return tp_all_gather(result_mine, core_bit, chip_bit)

    firsts = [attention(hidden_in[p], lengths[p]) for p in range(prompt_batch)]
    first_attended, ffn_all = lax.optimization_barrier((firsts[0][1], ffn_all))
    gate_up_weight = ffn_all[:, : 2 * ff_cols]
    down_weight = ffn_all[:, 2 * ff_cols :].reshape(req_count, -1).reshape(-1, model_cols)
    results = []
    for p, (flat_rows, attended, _) in enumerate(firsts):
        if p == 0:
            attended = first_attended
        results.append(finish(flat_rows, attended, gate_up_weight, down_weight))
    hidden_out = jnp.stack(results)
    kv_cache = jnp.stack([cache for _, _, cache in firsts])
    return (hidden_out, kv_cache)


def solution(mesh):
    placed = (
        P("req", None, None),
        P("req"),
        P(),
        P(),
        P(("req", "tp"), None),
        P(("req", "tp"), None),
        P(("req", "tp"), None),
        P(("req", "tp"), None),
        P(("req", "tp"), None),
        P(("req", "tp"), None),
        P(("req", "tp"), None),
    )
    return jax.shard_map(
        local,
        mesh=mesh,
        in_specs=placed,
        out_specs=(P("req", None, None), P("req", None, None)),
        check_vma=False,
    )
```

```python
import math

import jax
import jax.numpy as jnp
from jax import lax
from jax.experimental import pallas as pl
from jax.experimental.pallas import tpu as pltpu
from jax.sharding import PartitionSpec as P

QUERY_HEADS = 20
KEY_VALUE_HEADS = 5
HEAD_DIM = 64


def rms_norm(field, gain_vec):
    scale = lax.rsqrt(jnp.mean(field * field, axis=-1, keepdims=True) + 1e-05)
    return (field * scale * gain_vec).astype(jnp.bfloat16)


def rope_tables(sequence_length, head_size):
    half_width = head_size // 2
    positions = jnp.arange(sequence_length, dtype=jnp.float32)[:, None]
    frequency = jnp.exp(
        -math.log(10000.0) * (2.0 * jnp.arange(half_width, dtype=jnp.float32) / head_size)
    )
    angles = positions * frequency[None, :]
    return (jnp.cos(angles), jnp.sin(angles))


def rotate(field, cosine_table, sine_table):
    half_width = field.shape[-1] // 2
    first_half = field[..., :half_width]
    second_half = field[..., half_width:]
    cos_b = cosine_table[:, None, :]
    sin_b = sine_table[:, None, :]
    return jnp.concatenate(
        [first_half * cos_b - second_half * sin_b, second_half * cos_b + first_half * sin_b],
        axis=-1,
    )


REQ_DIMS = (4, 4, 2)
CHIP_PAIRS = [(0, 1), (1, 0), (2, 3), (3, 2)]
CROSS_PAIRS = [(0, 2), (2, 0), (1, 3), (3, 1)]


def _attn_body(len_ref, q_ref, k_ref, v_ref, o_ref):
    n = q_ref.shape[0]
    row = lax.broadcasted_iota(jnp.int32, (n, n), 0)
    col = lax.broadcasted_iota(jnp.int32, (n, n), 1)
    allowed = (col <= row) & (col < len_ref[0])
    for h in range(q_ref.shape[1] // HEAD_DIM):
        cols = slice(h * HEAD_DIM, (h + 1) * HEAD_DIM)
        q = q_ref[:, cols]
        k = k_ref[:, cols]
        v = v_ref[:, cols]
        s = lax.dot_general(q, k, (((1,), (1,)), ((), ())), preferred_element_type=jnp.float32) / 8.0
        s = jnp.where(allowed, s, -1e30)
        m = jnp.max(s, axis=-1, keepdims=True)
        e = jnp.exp(s - m)
        w = (e / jnp.sum(e, axis=-1, keepdims=True)).astype(jnp.bfloat16)
        o_ref[:, cols] = jnp.dot(w, v, preferred_element_type=jnp.float32).astype(o_ref.dtype)


def causal_attention(q, k, v, length, interpret=False):
    n, width = q.shape
    full = pl.BlockSpec((n, width), lambda i, ln: (0, 0))
    return pl.pallas_call(
        _attn_body,
        grid_spec=pltpu.PrefetchScalarGridSpec(
            num_scalar_prefetch=1, grid=(1,), in_specs=[full, full, full], out_specs=full
        ),
        out_shape=jax.ShapeDtypeStruct((n, width), jnp.bfloat16),
        interpret=interpret,
    )(length.reshape(1), q, k, v)


def pick(stack, index):
    return lax.dynamic_index_in_dim(stack, index, axis=0, keepdims=False)


def tp_reduce_scatter(partial, core_bit, chip_bit):
    rows, width = partial.shape
    halves = partial.reshape(2, rows // 2, width)
    got = lax.ppermute(pick(halves, 1 - core_bit), "tp", CHIP_PAIRS)
    first = pick(halves, core_bit).astype(jnp.float32) + got.astype(jnp.float32)
    quarters = first.reshape(2, rows // 4, width)
    sent = pick(quarters, 1 - chip_bit).astype(jnp.bfloat16)
    got = lax.ppermute(sent, "tp", CROSS_PAIRS)
    return pick(quarters, chip_bit) + got.astype(jnp.float32)


def tp_all_gather(quarter, core_bit, chip_bit):
    got = lax.ppermute(quarter, "tp", CROSS_PAIRS)
    half = jnp.zeros((2,) + quarter.shape, quarter.dtype)
    half = lax.dynamic_update_index_in_dim(half, quarter, chip_bit, 0)
    half = lax.dynamic_update_index_in_dim(half, got, 1 - chip_bit, 0)
    half = half.reshape((-1,) + quarter.shape[1:])
    got = lax.ppermute(half, "tp", CHIP_PAIRS)
    full = jnp.zeros((2,) + half.shape, half.dtype)
    full = lax.dynamic_update_index_in_dim(full, half, core_bit, 0)
    full = lax.dynamic_update_index_in_dim(full, got, 1 - core_bit, 0)
    return full.reshape((-1,) + half.shape[1:])


def ring_step(block, pos, size, shift_pairs):
    up, down = shift_pairs
    buf = jnp.zeros((size,) + block.shape, block.dtype)
    buf = lax.dynamic_update_index_in_dim(buf, block, pos, 0)
    from_below = lax.ppermute(block, "req", up)
    from_above = lax.ppermute(block, "req", down)
    buf = lax.dynamic_update_index_in_dim(buf, from_below, (pos + size - 1) % size, 0)
    buf = lax.dynamic_update_index_in_dim(buf, from_above, (pos + 1) % size, 0)
    half = block.shape[0] // 2
    far_low = lax.ppermute(from_below[:half], "req", up)
    far_high = lax.ppermute(from_above[half:], "req", down)
    far = jnp.concatenate([far_low, far_high], axis=0)
    buf = lax.dynamic_update_index_in_dim(buf, far, (pos + 2) % size, 0)
    return buf.reshape((size * block.shape[0],) + block.shape[1:])


def req_gather_stages(req_index, dims):
    nz, nx, ny = dims
    z = req_index // (nx * ny)
    x = (req_index // ny) % nx
    y = req_index % ny
    ids = [(a, b, c) for a in range(nz) for b in range(nx) for c in range(ny)]

    def lin(a, b, c):
        return (a * nx + b) * ny + c

    y_pairs = [(lin(a, b, c), lin(a, b, 1 - c)) for a, b, c in ids]
    x_pairs = (
        [(lin(a, b, c), lin(a, (b + 1) % nx, c)) for a, b, c in ids],
        [(lin(a, b, c), lin(a, (b - 1) % nx, c)) for a, b, c in ids],
    )
    z_pairs = (
        [(lin(a, b, c), lin((a + 1) % nz, b, c)) for a, b, c in ids],
        [(lin(a, b, c), lin((a - 1) % nz, b, c)) for a, b, c in ids],
    )

    def y_stage(block):
        got = lax.ppermute(block, "req", y_pairs)
        return jnp.where(
            y == 0, jnp.concatenate([block, got], 0), jnp.concatenate([got, block], 0)
        )

    def x_stage(block):
        return ring_step(block, x, nx, x_pairs)

    def z_stage(block):
        return ring_step(block, z, nz, z_pairs)

    return y_stage, x_stage, z_stage


def local(
    hidden_in,
    lengths,
    attn_gain,
    mlp_gain,
    q_master,
    k_master,
    trainer_value_weight,
    o_master,
    gate_master,
    up_master,
    down_master,
):
    tp_count = lax.axis_size("tp")
    req_count = lax.axis_size("req")
    tensor_shard_index = lax.axis_index("tp")
    core_bit = tensor_shard_index % 2
    chip_bit = tensor_shard_index // 2
    bf = jnp.bfloat16
    q_cols = q_master.shape[1] // tp_count
    kv_cols = k_master.shape[1]
    ff_cols = gate_master.shape[1] // tp_count
    local_rows = q_master.shape[0]
    model_cols = o_master.shape[1]
    block_rows = tp_count * local_rows

    def dest_chunk(dest):
        return jnp.concatenate(
            [
                q_master[:, dest * q_cols : (dest + 1) * q_cols],
                k_master,
                trainer_value_weight,
                gate_master[:, dest * ff_cols : (dest + 1) * ff_cols],
                up_master[:, dest * ff_cols : (dest + 1) * ff_cols],
            ],
            axis=1,
        ).astype(bf)

    send = jnp.stack([dest_chunk(d) for d in range(tp_count)])
    recv = lax.all_to_all(send, "tp", 0, 0, tiled=False)
    col_block = recv.reshape(block_rows, -1)
    qkv_width = q_cols + 2 * kv_cols

    o_size = o_master.size
    row_pack = jnp.concatenate([o_master.reshape(-1), down_master.reshape(-1)]).astype(bf)
    per_block = req_count // tp_count
    perm = []
    for r_src in range(req_count):
        for t_src in range(tp_count):
            r_dst = tp_count * (r_src % per_block) + t_src
            t_dst = r_src // per_block
            perm.append((r_src * tp_count + t_src, r_dst * tp_count + t_dst))
    row_pack = lax.ppermute(row_pack, ("req", "tp"), perm)

    attn_pack = jnp.concatenate(
        [col_block[:, :qkv_width], row_pack[:o_size].reshape(block_rows, -1)], axis=1
    )
    ffn_pack = jnp.concatenate(
        [col_block[:, qkv_width:], row_pack[o_size:].reshape(block_rows, -1)], axis=1
    )
    y_stage, x_stage, z_stage = req_gather_stages(lax.axis_index("req"), REQ_DIMS)
    attn_y = y_stage(attn_pack)
    ffn_y = y_stage(ffn_pack)
    attn_x = x_stage(attn_y)
    ffn_z = z_stage(ffn_y)
    attn_all = z_stage(attn_x)
    ffn_xz = x_stage(ffn_z)
    nz, nx, _ = REQ_DIMS
    ffn_all = (
        ffn_xz.reshape((nx, nz, -1) + ffn_xz.shape[1:])
        .transpose(1, 0, 2, 3)
        .reshape(ffn_xz.shape)
    )
    qkv_weight = attn_all[:, :qkv_width]
    out_weight = attn_all[:, qkv_width:].reshape(req_count, -1).reshape(-1, model_cols)

    prompt_batch, sequence_length, model_width = hidden_in.shape
    local_heads = q_cols // HEAD_DIM
    cosine_table, sine_table = rope_tables(sequence_length, HEAD_DIM)
    owner_shards = (
        tensor_shard_index * local_heads + jnp.arange(local_heads, dtype=jnp.int32)
    ) // (QUERY_HEADS // KEY_VALUE_HEADS)
    quarter_rows = sequence_length // tp_count
    row_start = (core_bit * 2 + chip_bit) * quarter_rows

    def attention(prompt_rows, length):
        flat_rows = prompt_rows.astype(jnp.float32)
        normalized_input = rms_norm(flat_rows, attn_gain)
        qkv = jnp.dot(normalized_input, qkv_weight, preferred_element_type=jnp.float32)
        queries = qkv[:, :q_cols].reshape(sequence_length, local_heads, HEAD_DIM)
        key_rows = qkv[:, q_cols : q_cols + kv_cols].reshape(
            sequence_length, KEY_VALUE_HEADS, HEAD_DIM
        )
        value_rows = qkv[:, q_cols + kv_cols :].reshape(sequence_length, KEY_VALUE_HEADS, HEAD_DIM)
        q_rot = rotate(queries, cosine_table, sine_table).astype(jnp.bfloat16)
        rotated_keys = rotate(key_rows, cosine_table, sine_table).astype(jnp.bfloat16)
        value_halves = value_rows.astype(jnp.bfloat16)
        cache = jnp.concatenate(
            [
                rotated_keys.reshape(sequence_length, KEY_VALUE_HEADS * HEAD_DIM),
                value_halves.reshape(sequence_length, KEY_VALUE_HEADS * HEAD_DIM),
            ],
            axis=1,
        )
        attended = causal_attention(
            q_rot.reshape(sequence_length, -1),
            jnp.take(rotated_keys, owner_shards, axis=1).reshape(sequence_length, -1),
            jnp.take(value_halves, owner_shards, axis=1).reshape(sequence_length, -1),
            length,
        )
        return flat_rows, attended, cache

    def finish(flat_rows, attended, gate_up_weight, down_weight):
        attn_partial = jnp.dot(attended, out_weight, preferred_element_type=jnp.float32).astype(bf)
        attn_mine = tp_reduce_scatter(attn_partial, core_bit, chip_bit)
        middle = lax.dynamic_slice_in_dim(flat_rows, row_start, quarter_rows, 0) + attn_mine
        normed_mine = rms_norm(middle, mlp_gain)
        normed_rows = tp_all_gather(normed_mine, core_bit, chip_bit)
        gate_up = jnp.dot(normed_rows, gate_up_weight, preferred_element_type=jnp.float32)
        gate_val = gate_up[:, :ff_cols]
        up_val = gate_up[:, ff_cols:]
        hidden_ff = (jax.nn.silu(gate_val) * up_val).astype(jnp.bfloat16)
        ffn_partial = jnp.dot(hidden_ff, down_weight, preferred_element_type=jnp.float32).astype(bf)
        ffn_mine = tp_reduce_scatter(ffn_partial, core_bit, chip_bit)
        result_mine = (middle + ffn_mine).astype(jnp.bfloat16)
        return tp_all_gather(result_mine, core_bit, chip_bit)

    firsts = [attention(hidden_in[p], lengths[p]) for p in range(prompt_batch)]
    first_attended, ffn_all = lax.optimization_barrier((firsts[0][1], ffn_all))
    gate_up_weight = ffn_all[:, : 2 * ff_cols]
    down_weight = ffn_all[:, 2 * ff_cols :].reshape(req_count, -1).reshape(-1, model_cols)
    results = []
    for p, (flat_rows, attended, _) in enumerate(firsts):
        if p == 0:
            attended = first_attended
        results.append(finish(flat_rows, attended, gate_up_weight, down_weight))
    hidden_out = jnp.stack(results)
    kv_cache = jnp.stack([cache for _, _, cache in firsts])
    return (hidden_out, kv_cache)


def solution(mesh):
    placed = (
        P("req", None, None),
        P("req"),
        P(),
        P(),
        P(("req", "tp"), None),
        P(("req", "tp"), None),
        P(("req", "tp"), None),
        P(("req", "tp"), None),
        P(("req", "tp"), None),
        P(("req", "tp"), None),
        P(("req", "tp"), None),
    )
    return jax.shard_map(
        local,
        mesh=mesh,
        in_specs=placed,
        out_specs=(P("req", None, None), P("req", None, None)),
        check_vma=False,
    )
```
